128 devices in a mesh: blk: 32 (over y, z, core), lvl: 4 (over x).
Axes of the slice: x: 4, y: 4, z: 4, core: 2. Of those that a mesh axis runs over, the one named last changes fastest.
Arguments:
- rhs: bfloat16 [4, 32, 768, 384], P('lvl', 'blk'), may hold values from -6 to 6
- inverse: bfloat16 [4, 32, 768, 768], P('lvl', 'blk'), may hold values from -1 to 3
- left_factors: bfloat16 [4, 32, 4, 768, 128], P('lvl', 'blk'), may hold values from -0.1875 to 0.1875
- right_factors: bfloat16 [4, 32, 4, 768, 128], P('lvl', 'blk'), may hold values from -0.21875 to 0.21875
- sources: int32 [4, 32, 4], replicated, may hold values from 0 to 31, as said below
- ranks: int32 [4, 32, 4], replicated, may hold values from 32 to 128
- owner: int32 [4, 32], replicated, may hold values from 0 to 31, as said below
Outputs:
- forward: bfloat16 [4, 32, 768, 384], P('lvl', 'blk')
- backward: bfloat16 [4, 32, 768, 384], P('lvl', 'blk')
The draws below stay inside these ranges and needn't reach their ends.
Inputs may be any that keep to these rules, and one draw needn't show every extreme that they name: Every row owner[l] is a permutation of the positions; position p is stored on blk index p. sources[l] names blocks of level l - 1 (the row of level 0 names blocks of the last level and is unused); for each level and each k, column k names every block once; between consecutive levels the tiles from the blocks of one blk index to those of another number 0 or exactly 1.
All inputs are finite; a program needn't handle non-finite values.
Results may differ from the reference program's by a relative error of at most 0.02.
Values may be sent and summed in bfloat16 or wider, within the bound.
No kernel may reach another device: no remote copies, remote signals or barrier semaphores. Data moves between devices by JAX's collectives and lax.ppermute only.
A program may use at most 64 MiB of HBM per device.

```python
import math
import jax
import jax.numpy as jnp
from jax import lax

BLOCK = 768
RHS = 384
RANK = 128
TILES = 4
BLK_DEV = 1
LEVELS = 4
NBLOCKS = 32


def routing_draw(key):
    device_count = NBLOCKS // BLK_DEV
    position = jnp.arange(NBLOCKS, dtype=jnp.int32)
    owners = []
    holders = []
    row_perms = []
    col_perms = []
    symbol_perms = []
    for section_at in range(LEVELS):
        placed = jax.random.permutation(jax.random.fold_in(key, 17 + section_at), NBLOCKS).astype(jnp.int32)
        owners.append(placed)
        holders.append(jnp.zeros((NBLOCKS,), jnp.int32).at[placed].set(position))
        row_perms.append(jax.random.permutation(jax.random.fold_in(key, 301 + section_at), device_count).astype(jnp.int32))
        col_perms.append(jax.random.permutation(jax.random.fold_in(key, 601 + section_at), device_count).astype(jnp.int32))
        symbol_perms.append(jax.random.permutation(jax.random.fold_in(key, 901 + section_at), device_count).astype(jnp.int32))
    lane_ids = jnp.arange(TILES, dtype=jnp.int32)
    named = []
    for section_at in range(LEVELS):
        placed = owners[section_at]
        device_of = placed // BLK_DEV
        slot_of = placed % BLK_DEV
        lane_number = slot_of[:, None] * TILES + lane_ids[None, :]
        row_of = row_perms[section_at][lane_number % device_count]
        col_of = col_perms[section_at][device_of][:, None]
        src_dev = symbol_perms[section_at][(row_of + col_of) % device_count]
        src_slot = (slot_of[:, None] + lane_ids[None, :]) % BLK_DEV
        src_pos = src_dev * BLK_DEV + src_slot
        named.append(holders[(section_at - 1) % LEVELS][src_pos])
    return (jnp.stack(owners).astype(jnp.int32), jnp.stack(named).astype(jnp.int32))


def draw_owner(key, part):
    return routing_draw(key)[0]


def draw_sources(key, part):
    return routing_draw(key)[1]


def draw_inverse(key, part):
    shape = (LEVELS, NBLOCKS, BLOCK, BLOCK)
    row_ids = jnp.arange(BLOCK)
    identity = (row_ids[:, None] == row_ids[None, :]).astype(jnp.float32)
    noise = jax.random.normal(key, shape, jnp.float32) * (0.6 / math.sqrt(BLOCK))
    return (identity + noise).astype(jnp.bfloat16)


def with_ends(entries, rng, smallest, top_value):
    shape = entries.shape
    index_at = [jax.random.randint(jax.random.fold_in(rng, axis), (), 0, shape[axis]) for axis in range(len(shape))]
    entries = entries.at[tuple(index_at)].set(smallest)
    longest = shape.index(max(shape))
    index_at[longest] = (index_at[longest] + 1) % shape[longest]
    return entries.at[tuple(index_at)].set(top_value)


def steps_of(own_key, shape, pieces, least, top_value):
    loudness, own = 1.0, jax.random.fold_in(own_key, 6)
    for axis_at, parts in pieces:
        steps = jnp.exp(jax.random.uniform(jax.random.fold_in(own, axis_at), (parts,), jnp.float32, least / len(pieces), top_value / len(pieces)))
        loudness = loudness * jnp.repeat(steps, shape[axis_at] // parts).reshape([-1 if axis == axis_at else 1 for axis in range(len(shape))])
    return loudness


def scatter_about(rng, extent, scale, most, pieces=(), held_as=jnp.bfloat16):
    values = scale * jax.random.normal(rng, extent, jnp.float32)
    if pieces:
        values = values * steps_of(rng, extent, pieces, -0.22, 0.18)
    return jnp.clip(values, -most, most).astype(held_as)


def setup_inputs(seed: int = 0) -> dict:
    keys = jax.random.split(jax.random.key(seed), 8)
    rhs = scatter_about(keys[0], (LEVELS, NBLOCKS, BLOCK, RHS), 1.0, 6.0, ((0, 4), (1, 32)))
    inverse = draw_inverse(jax.random.fold_in(keys[7], 71), 0)
    left_factors = scatter_about(keys[2], (LEVELS, NBLOCKS, TILES, BLOCK, RANK), (2 * TILES * RANK) ** -0.5, 0.1875, ((0, 4), (1, 32)))
    right_factors = scatter_about(keys[3], (LEVELS, NBLOCKS, TILES, BLOCK, RANK), BLOCK ** -0.5, 0.21875, ((0, 4), (1, 32)))
    sources = draw_sources(jax.random.fold_in(keys[7], 71), 0)
    ranks = with_ends(jax.random.randint(keys[5], (LEVELS, NBLOCKS, TILES), RANK // 4, RANK + 1), jax.random.fold_in(keys[5], 1), RANK // 4, RANK).astype(jnp.int32)
    owner = draw_owner(jax.random.fold_in(keys[7], 71), 0)
    return {"rhs": rhs, "inverse": inverse, "left_factors": left_factors, "right_factors": right_factors, "sources": sources, "ranks": ranks, "owner": owner}


def level_maps(sources, owner, ranks, section_at):
    block_count = owner.shape[1]
    position = jnp.arange(block_count, dtype=jnp.int32)
    holder = jnp.zeros((block_count,), jnp.int32).at[owner[section_at].astype(jnp.int32)].set(position)
    src_block = sources[section_at][holder].astype(jnp.int32)
    src_pos = owner[section_at - 1][src_block].astype(jnp.int32)
    rank_pos = ranks[section_at][holder].astype(jnp.int32)
    columns = jnp.broadcast_to(jnp.arange(src_pos.shape[1], dtype=jnp.int32)[None, :], src_pos.shape)
    targets = jnp.broadcast_to(position[:, None], src_pos.shape)
    target_of = jnp.zeros(src_pos.shape, jnp.int32).at[src_pos, columns].set(targets)
    return src_pos, rank_pos, columns, target_of


def rank_mask(rank_pos, width):
    return (jnp.arange(width, dtype=jnp.int32)[None, None, :] < rank_pos[:, :, None]).astype(jnp.float32)


def reference(rhs, inverse, left_factors, right_factors, sources, ranks, owner):
    solved = []
    for section_at in range(LEVELS):
        current = rhs[section_at].astype(jnp.float32)
        if section_at > 0:
            src_pos, rank_pos, columns, target_of = level_maps(sources, owner, ranks, section_at)
            earlier = lax.optimization_barrier(solved[section_at - 1]).astype(jnp.float32)
            coef_src = jnp.einsum('skbr,sbn->skrn', right_factors[section_at - 1].astype(jnp.float32), earlier).astype(jnp.bfloat16)
            gathered = lax.optimization_barrier(coef_src)[src_pos, columns].astype(jnp.float32)
            gathered = gathered * rank_mask(rank_pos, RANK)[..., None]
            current = current - jnp.einsum('pkbr,pkrn->pbn', left_factors[section_at].astype(jnp.float32), gathered)
        rounded = lax.optimization_barrier(current.astype(jnp.bfloat16)).astype(jnp.float32)
        solved.append(jnp.einsum('pab,pbn->pan', inverse[section_at].astype(jnp.float32), rounded).astype(jnp.bfloat16))
    answer = [None] * LEVELS
    for section_at in reversed(range(LEVELS)):
        current = lax.optimization_barrier(solved[section_at]).astype(jnp.float32)
        if section_at < LEVELS - 1:
            src_pos, rank_pos, columns, target_of = level_maps(sources, owner, ranks, section_at + 1)
            higher = lax.optimization_barrier(answer[section_at + 1]).astype(jnp.float32)
            outgoing = jnp.einsum('pkbr,pbn->pkrn', left_factors[section_at + 1].astype(jnp.float32), higher)
            outgoing = (outgoing * rank_mask(rank_pos, RANK)[..., None]).astype(jnp.bfloat16)
            arrived = lax.optimization_barrier(outgoing)[target_of, columns].astype(jnp.float32)
            current = current - jnp.einsum('skbr,skrn->sbn', right_factors[section_at].astype(jnp.float32), arrived)
        rounded = lax.optimization_barrier(current.astype(jnp.bfloat16)).astype(jnp.float32)
        answer[section_at] = jnp.einsum('pba,pbn->pan', inverse[section_at].astype(jnp.float32), rounded).astype(jnp.bfloat16)
    return jnp.stack(solved), jnp.stack(answer)
```

```python
import jax
import jax.numpy as jnp
from jax import lax
from jax.sharding import PartitionSpec as P


def routing_tables(sources, owner, ranks):
    level_count, block_count = owner.shape
    position = jnp.arange(block_count, dtype=jnp.int32)
    tables = [None]
    for t in range(1, level_count):
        at_pos = (owner[t][None, :] == position[:, None]).astype(jnp.int32)
        src_block = jnp.sum(at_pos[:, :, None] * sources[t][None, :, :], axis=1)
        rank_pos = jnp.sum(at_pos[:, :, None] * ranks[t][None, :, :], axis=1)
        pick = (src_block[:, :, None] == position[None, None, :]).astype(jnp.int32)
        src_pos = jnp.sum(pick * owner[t - 1][None, None, :], axis=2)
        hit = (src_pos[:, None, :] == position[None, :, None]).astype(jnp.int32)
        target_of = jnp.sum(hit * position[:, None, None], axis=0)
        tables.append((src_pos, rank_pos, target_of))
    return tables


def mine(table, me):
    block_count = table.shape[0]
    row = (jnp.arange(block_count, dtype=jnp.int32) == me).astype(jnp.int32)
    return jnp.sum(row[:, None] * table, axis=0)


def one_hot(index, count, dtype):
    return (index[:, None] == jnp.arange(count, dtype=jnp.int32)[None, :]).astype(dtype)


def spread(out, src_row, row_count, my_row):
    width = out.shape[-1] // row_count
    piece = None
    for r in range(row_count):
        part = out[..., r * width:(r + 1) * width]
        if r == src_row:
            got = jnp.where(my_row == r, part, jnp.zeros_like(part))
        else:
            got = lax.ppermute(part, "lvl", [(src_row, r)])
        piece = got if piece is None else piece + got
    return piece


def collect(routed, dst_row, row_count):
    parts = []
    for r in range(row_count):
        if r == dst_row:
            parts.append(routed)
        else:
            parts.append(lax.ppermute(routed, "lvl", [(r, dst_row)]))
    return jnp.concatenate(parts, axis=-1)


def route(piece, send_to, take_from, block_count):
    send = one_hot(send_to, block_count, piece.dtype)
    holder = jnp.einsum("kj,krn->jrn", send, piece, preferred_element_type=jnp.float32)
    holder = holder.astype(piece.dtype)
    arrived = lax.all_to_all(holder, "blk", split_axis=0, concat_axis=0, tiled=True)
    take = one_hot(take_from, block_count, piece.dtype)
    routed = jnp.einsum("kj,jrn->krn", take, arrived, preferred_element_type=jnp.float32)
    return routed.astype(piece.dtype)


def local(rhs, inverse, left_factors, right_factors, sources, ranks, owner):
    assert rhs.shape[1] == 1
    level_count = sources.shape[0]
    block_count = owner.shape[1]
    row_count = lax.axis_size("lvl")
    rank_width = left_factors.shape[4]
    rhs_here = rhs[0, 0]
    inverse_here = inverse[0, 0]
    left_here = left_factors[0, 0]
    right_here = right_factors[0, 0]
    my_row = lax.axis_index("lvl")
    me = lax.axis_index("blk")
    tables = routing_tables(sources, owner, ranks)
    mine_src = [None] + [mine(tables[t][0], me) for t in range(1, level_count)]
    mine_rank = [None] + [mine(tables[t][1], me) for t in range(1, level_count)]
    mine_target = [None] + [mine(tables[t][2], me) for t in range(1, level_count)]
    lanes = jnp.arange(rank_width, dtype=jnp.int32)

    def keep_of(t):
        return (lanes[None, :] < mine_rank[t][:, None]).astype(jnp.float32)

    solved = jnp.zeros(rhs_here.shape, jnp.bfloat16)
    incoming = None
    for t in range(level_count):
        current = rhs_here.astype(jnp.float32)
        if t > 0:
            masked = incoming * keep_of(t)[..., None].astype(jnp.bfloat16)
            current = current - jnp.einsum(
                "kbr,krn->bn", left_here, masked, preferred_element_type=jnp.float32
            )
        lowered = current.astype(jnp.bfloat16)
        result = jnp.einsum(
            "ab,bn->an", inverse_here, lowered, preferred_element_type=jnp.float32
        ).astype(jnp.bfloat16)
        solved = jnp.where(my_row == t, result, solved)
        if t + 1 < level_count:
            out = jnp.einsum(
                "kbr,bn->krn", right_here, result, preferred_element_type=jnp.float32
            ).astype(jnp.bfloat16)
            piece = spread(out, t, row_count, my_row)
            routed = route(piece, mine_target[t + 1], mine_src[t + 1], block_count)
            incoming = collect(routed, t + 1, row_count)

    answer = jnp.zeros(rhs_here.shape, jnp.bfloat16)
    returning = None
    for t in reversed(range(level_count)):
        current = solved.astype(jnp.float32)
        if t + 1 < level_count:
            current = current - jnp.einsum(
                "kbr,krn->bn", right_here, returning, preferred_element_type=jnp.float32
            )
        upper = current.astype(jnp.bfloat16)
        result = jnp.einsum(
            "ba,bn->an", inverse_here, upper, preferred_element_type=jnp.float32
        ).astype(jnp.bfloat16)
        answer = jnp.where(my_row == t, result, answer)
        if t > 0:
            projected = jnp.einsum(
                "kbr,bn->krn", left_here, result, preferred_element_type=jnp.float32
            )
            out = (projected * keep_of(t)[..., None]).astype(jnp.bfloat16)
            piece = spread(out, t, row_count, my_row)
            routed = route(piece, mine_src[t], mine_target[t], block_count)
            returning = collect(routed, t - 1, row_count)
    return (solved[None, None], answer[None, None])


def solution(mesh):
    return jax.shard_map(
        local,
        mesh=mesh,
        in_specs=(
            P("lvl", "blk", None, None),
            P("lvl", "blk", None, None),
            P("lvl", "blk", None, None, None),
            P("lvl", "blk", None, None, None),
            P(),
            P(),
            P(),
        ),
        out_specs=(P("lvl", "blk", None, None), P("lvl", "blk", None, None)),
        check_vma=False,
    )
```

```python
import jax
import jax.numpy as jnp
from jax import lax
from jax.sharding import PartitionSpec as P


def routing_tables(sources, owner, ranks):
    level_count, block_count = owner.shape
    position = jnp.arange(block_count, dtype=jnp.int32)
    tables = [None]
    for t in range(1, level_count):
        at_pos = (owner[t][None, :] == position[:, None]).astype(jnp.int32)
        src_block = jnp.sum(at_pos[:, :, None] * sources[t][None, :, :], axis=1)
        rank_pos = jnp.sum(at_pos[:, :, None] * ranks[t][None, :, :], axis=1)
        pick = (src_block[:, :, None] == position[None, None, :]).astype(jnp.int32)
        src_pos = jnp.sum(pick * owner[t - 1][None, None, :], axis=2)
        hit = (src_pos[:, None, :] == position[None, :, None]).astype(jnp.int32)
        target_of = jnp.sum(hit * position[:, None, None], axis=0)
        tables.append((src_pos, rank_pos, target_of))
    return tables


def mine(table, me):
    block_count = table.shape[0]
    row = (jnp.arange(block_count, dtype=jnp.int32) == me).astype(jnp.int32)
    return jnp.sum(row[:, None] * table, axis=0)


def one_hot(index, count, dtype):
    return (index[:, None] == jnp.arange(count, dtype=jnp.int32)[None, :]).astype(dtype)


def hops(a, b, row_count):
    d = (b - a) % row_count
    return min(d, row_count - d)


def spread(out, src_row, row_count, my_row):
    width = out.shape[-1] // row_count
    piece = None
    for r in sorted(range(row_count), key=lambda r: -hops(src_row, r, row_count)):
        part = out[..., r * width:(r + 1) * width]
        if r == src_row:
            got = jnp.where(my_row == r, part, jnp.zeros_like(part))
        else:
            got = lax.ppermute(part, "lvl", [(src_row, r)])
        piece = got if piece is None else piece + got
    return piece


def collect(routed, dst_row, row_count):
    parts = [None] * row_count
    for r in sorted(range(row_count), key=lambda r: -hops(r, dst_row, row_count)):
        if r == dst_row:
            parts[r] = routed
        else:
            parts[r] = lax.ppermute(routed, "lvl", [(r, dst_row)])
    return jnp.concatenate(parts, axis=-1)


def route(piece, send_to, take_from, block_count):
    send = one_hot(send_to, block_count, piece.dtype)
    holder = jnp.einsum("kj,krn->jrn", send, piece, preferred_element_type=jnp.float32)
    holder = holder.astype(piece.dtype)
    arrived = lax.all_to_all(holder, "blk", split_axis=0, concat_axis=0, tiled=True)
    take = one_hot(take_from, block_count, piece.dtype)
    routed = jnp.einsum("kj,jrn->krn", take, arrived, preferred_element_type=jnp.float32)
    return routed.astype(piece.dtype)


def local(rhs, inverse, left_factors, right_factors, sources, ranks, owner):
    assert rhs.shape[1] == 1
    level_count = sources.shape[0]
    block_count = owner.shape[1]
    row_count = lax.axis_size("lvl")
    rank_width = left_factors.shape[4]
    rhs_here = rhs[0, 0]
    inverse_here = inverse[0, 0]
    left_here = left_factors[0, 0]
    right_here = right_factors[0, 0]
    my_row = lax.axis_index("lvl")
    me = lax.axis_index("blk")
    tables = routing_tables(sources, owner, ranks)
    mine_src = [None] + [mine(tables[t][0], me) for t in range(1, level_count)]
    mine_rank = [None] + [mine(tables[t][1], me) for t in range(1, level_count)]
    mine_target = [None] + [mine(tables[t][2], me) for t in range(1, level_count)]
    lanes = jnp.arange(rank_width, dtype=jnp.int32)
    tile_count, block_rows, _ = left_here.shape
    my_rank = jnp.zeros((tile_count,), jnp.int32)
    for t in range(1, level_count):
        my_rank = jnp.where(my_row == t, mine_rank[t], my_rank)
    keep = (lanes[None, :] < my_rank[:, None]).astype(left_here.dtype)
    left_masked = left_here * keep[:, None, :]
    left_flat = left_masked.transpose(1, 0, 2).reshape(block_rows, tile_count * rank_width)
    right_flat = right_here.transpose(1, 0, 2).reshape(block_rows, tile_count * rank_width)
    inverse_t = inverse_here.T
    lane_shape = (tile_count, rank_width, rhs_here.shape[-1])

    solved = jnp.zeros(rhs_here.shape, jnp.bfloat16)
    incoming = None
    for t in range(level_count):
        current = rhs_here.astype(jnp.float32)
        if t > 0:
            current = current - jnp.dot(
                left_flat, incoming.reshape(-1, incoming.shape[-1]),
                preferred_element_type=jnp.float32,
            )
        lowered = current.astype(jnp.bfloat16)
        result = jnp.dot(
            inverse_here, lowered, preferred_element_type=jnp.float32
        ).astype(jnp.bfloat16)
        solved = jnp.where(my_row == t, result, solved)
        if t + 1 < level_count:
            out = jnp.einsum(
                "bm,bn->mn", right_flat, result, preferred_element_type=jnp.float32
            ).astype(jnp.bfloat16).reshape(lane_shape)
            piece = spread(out, t, row_count, my_row)
            routed = route(piece, mine_target[t + 1], mine_src[t + 1], block_count)
            incoming = collect(routed, t + 1, row_count)

    answer = jnp.zeros(rhs_here.shape, jnp.bfloat16)
    returning = None
    for t in reversed(range(level_count)):
        current = solved.astype(jnp.float32)
        if t + 1 < level_count:
            current = current - jnp.dot(
                right_flat, returning.reshape(-1, returning.shape[-1]),
                preferred_element_type=jnp.float32,
            )
        upper = current.astype(jnp.bfloat16)
        result = jnp.dot(
            inverse_t, upper, preferred_element_type=jnp.float32
        ).astype(jnp.bfloat16)
        answer = jnp.where(my_row == t, result, answer)
        if t > 0:
            out = jnp.einsum(
                "bm,bn->mn", left_flat, result, preferred_element_type=jnp.float32
            ).astype(jnp.bfloat16).reshape(lane_shape)
            piece = spread(out, t, row_count, my_row)
            routed = route(piece, mine_src[t], mine_target[t], block_count)
            returning = collect(routed, t - 1, row_count)
    return (solved[None, None], answer[None, None])


def solution(mesh):
    return jax.shard_map(
        local,
        mesh=mesh,
        in_specs=(
            P("lvl", "blk", None, None),
            P("lvl", "blk", None, None),
            P("lvl", "blk", None, None, None),
            P("lvl", "blk", None, None, None),
            P(),
            P(),
            P(),
        ),
        out_specs=(P("lvl", "blk", None, None), P("lvl", "blk", None, None)),
        check_vma=False,
    )
```

```python
import jax
import jax.numpy as jnp
from jax import lax
from jax.sharding import PartitionSpec as P


def routing_tables(sources, owner, ranks):
    level_count, block_count = owner.shape
    position = jnp.arange(block_count, dtype=jnp.int32)
    tables = [None]
    for t in range(1, level_count):
        at_pos = (owner[t][None, :] == position[:, None]).astype(jnp.int32)
        src_block = jnp.sum(at_pos[:, :, None] * sources[t][None, :, :], axis=1)
        rank_pos = jnp.sum(at_pos[:, :, None] * ranks[t][None, :, :], axis=1)
        pick = (src_block[:, :, None] == position[None, None, :]).astype(jnp.int32)
        src_pos = jnp.sum(pick * owner[t - 1][None, None, :], axis=2)
        hit = (src_pos[:, None, :] == position[None, :, None]).astype(jnp.int32)
        target_of = jnp.sum(hit * position[:, None, None], axis=0)
        tables.append((src_pos, rank_pos, target_of))
    return tables


def mine(table, me):
    block_count = table.shape[0]
    row = (jnp.arange(block_count, dtype=jnp.int32) == me).astype(jnp.int32)
    return jnp.sum(row[:, None] * table, axis=0)


def one_hot(index, count, dtype):
    return (index[:, None] == jnp.arange(count, dtype=jnp.int32)[None, :]).astype(dtype)


def spread(out, src_row, row_count, my_row):
    width = out.shape[-1] // row_count
    piece = None
    for r in range(row_count):
        part = out[..., r * width:(r + 1) * width]
        if r == src_row:
            got = jnp.where(my_row == r, part, jnp.zeros_like(part))
        else:
            got = lax.ppermute(part, "lvl", [(src_row, r)])
        piece = got if piece is None else piece + got
    return piece


def collect(routed, dst_row, row_count):
    parts = []
    for r in range(row_count):
        if r == dst_row:
            parts.append(routed)
        else:
            parts.append(lax.ppermute(routed, "lvl", [(r, dst_row)]))
    return jnp.concatenate(parts, axis=-1)


def route(piece, send_to, take_from, block_count):
    send = one_hot(send_to, block_count, piece.dtype)
    holder = jnp.einsum("kj,krn->jrn", send, piece, preferred_element_type=jnp.float32)
    holder = holder.astype(piece.dtype)
    arrived = lax.all_to_all(holder, "blk", split_axis=0, concat_axis=0, tiled=True)
    take = one_hot(take_from, block_count, piece.dtype)
    routed = jnp.einsum("kj,jrn->krn", take, arrived, preferred_element_type=jnp.float32)
    return routed.astype(piece.dtype)


def local(rhs, inverse, left_factors, right_factors, sources, ranks, owner):
    assert rhs.shape[1] == 1
    level_count = sources.shape[0]
    block_count = owner.shape[1]
    row_count = lax.axis_size("lvl")
    rank_width = left_factors.shape[4]
    rhs_here = rhs[0, 0]
    inverse_here = inverse[0, 0]
    left_here = left_factors[0, 0]
    right_here = right_factors[0, 0]
    my_row = lax.axis_index("lvl")
    me = lax.axis_index("blk")
    tables = routing_tables(sources, owner, ranks)
    mine_src = [None] + [mine(tables[t][0], me) for t in range(1, level_count)]
    mine_rank = [None] + [mine(tables[t][1], me) for t in range(1, level_count)]
    mine_target = [None] + [mine(tables[t][2], me) for t in range(1, level_count)]
    lanes = jnp.arange(rank_width, dtype=jnp.int32)

    def keep_of(t):
        return (lanes[None, :] < mine_rank[t][:, None]).astype(jnp.float32)

    solved = jnp.zeros(rhs_here.shape, jnp.bfloat16)
    own_blocks = []
    incoming = None
    for t in range(level_count):
        current = rhs_here.astype(jnp.float32)
        if t > 0:
            masked = incoming * keep_of(t)[..., None].astype(jnp.bfloat16)
            current = current - jnp.einsum(
                "kbr,krn->bn", left_here, masked, preferred_element_type=jnp.float32
            )
        lowered = current.astype(jnp.bfloat16)
        result = jnp.einsum(
            "ab,bn->an", inverse_here, lowered, preferred_element_type=jnp.float32
        ).astype(jnp.bfloat16)
        solved = jnp.where(my_row == t, result, solved)
        if t + 1 < level_count:
            own_blocks.append(spread(result, t, row_count, my_row))
            out = jnp.einsum(
                "kbr,bn->krn", right_here, result, preferred_element_type=jnp.float32
            ).astype(jnp.bfloat16)
            piece = spread(out, t, row_count, my_row)
            routed = route(piece, mine_target[t + 1], mine_src[t + 1], block_count)
            incoming = collect(routed, t + 1, row_count)

    last = level_count - 1
    width = rhs_here.shape[-1] // row_count
    inverse_all = lax.all_gather(inverse_here, "lvl")
    right_all = lax.all_gather(right_here, "lvl")
    left_all = lax.all_gather(left_here, "lvl")

    result = jnp.einsum(
        "ba,bn->an", inverse_here, solved, preferred_element_type=jnp.float32
    ).astype(jnp.bfloat16)
    top = result
    projected = jnp.einsum(
        "kbr,bn->krn", left_here, result, preferred_element_type=jnp.float32
    )
    out = (projected * keep_of(last)[..., None]).astype(jnp.bfloat16)
    piece = spread(out, last, row_count, my_row)
    returning = route(piece, mine_src[last], mine_target[last], block_count)
    blocks = [None] * level_count
    for t in reversed(range(last)):
        current = own_blocks[t].astype(jnp.float32) - jnp.einsum(
            "kbr,krn->bn", right_all[t], returning, preferred_element_type=jnp.float32
        )
        upper = current.astype(jnp.bfloat16)
        result = jnp.einsum(
            "ba,bn->an", inverse_all[t], upper, preferred_element_type=jnp.float32
        ).astype(jnp.bfloat16)
        blocks[t] = result
        if t > 0:
            projected = jnp.einsum(
                "kbr,bn->krn", left_all[t], result, preferred_element_type=jnp.float32
            )
            out = (projected * keep_of(t)[..., None]).astype(jnp.bfloat16)
            returning = route(out, mine_src[t], mine_target[t], block_count)
    answer = top
    for t in range(last):
        answer = jnp.where(my_row == t, collect(blocks[t], t, row_count), answer)
    return (solved[None, None], answer[None, None])


def solution(mesh):
    return jax.shard_map(
        local,
        mesh=mesh,
        in_specs=(
            P("lvl", "blk", None, None),
            P("lvl", "blk", None, None),
            P("lvl", "blk", None, None, None),
            P("lvl", "blk", None, None, None),
            P(),
            P(),
            P(),
        ),
        out_specs=(P("lvl", "blk", None, None), P("lvl", "blk", None, None)),
        check_vma=False,
    )
```

```python
import jax
import jax.numpy as jnp
from jax import lax
from jax.sharding import PartitionSpec as P


def routing_tables(sources, owner, ranks):
    level_count, block_count = owner.shape
    position = jnp.arange(block_count, dtype=jnp.int32)
    tables = [None]
    for t in range(1, level_count):
        at_pos = (owner[t][None, :] == position[:, None]).astype(jnp.int32)
        src_block = jnp.sum(at_pos[:, :, None] * sources[t][None, :, :], axis=1)
        rank_pos = jnp.sum(at_pos[:, :, None] * ranks[t][None, :, :], axis=1)
        pick = (src_block[:, :, None] == position[None, None, :]).astype(jnp.int32)
        src_pos = jnp.sum(pick * owner[t - 1][None, None, :], axis=2)
        hit = (src_pos[:, None, :] == position[None, :, None]).astype(jnp.int32)
        target_of = jnp.sum(hit * position[:, None, None], axis=0)
        tables.append((src_pos, rank_pos, target_of))
    return tables


def mine(table, me):
    block_count = table.shape[0]
    row = (jnp.arange(block_count, dtype=jnp.int32) == me).astype(jnp.int32)
    return jnp.sum(row[:, None] * table, axis=0)


def one_hot(index, count, dtype):
    return (index[:, None] == jnp.arange(count, dtype=jnp.int32)[None, :]).astype(dtype)


def spread(out, src_row, row_count, my_row):
    width = out.shape[-1] // row_count
    piece = None
    for r in range(row_count):
        part = out[..., r * width:(r + 1) * width]
        if r == src_row:
            got = jnp.where(my_row == r, part, jnp.zeros_like(part))
        else:
            got = lax.ppermute(part, "lvl", [(src_row, r)])
        piece = got if piece is None else piece + got
    return piece


def collect(routed, dst_row, row_count):
    parts = []
    for r in range(row_count):
        if r == dst_row:
            parts.append(routed)
        else:
            parts.append(lax.ppermute(routed, "lvl", [(r, dst_row)]))
    return jnp.concatenate(parts, axis=-1)


def shift(array, by, row_count):
    return lax.ppermute(array, "lvl", [(i, (i + by) % row_count) for i in range(row_count)])


def one_hot_rows(index, count, dtype):
    return (jnp.arange(count, dtype=jnp.int32) == index).astype(dtype)


def blocks_of(level_blocks, my_row, by, row_count):
    wanted = lax.rem(my_row + by, row_count)
    chosen = level_blocks[0]
    for t in range(1, len(level_blocks)):
        chosen = jnp.where(wanted == t, level_blocks[t], chosen)
    return chosen


def route(piece, send_to, take_from, block_count):
    send = one_hot(send_to, block_count, piece.dtype)
    holder = jnp.einsum("kj,krn->jrn", send, piece, preferred_element_type=jnp.float32)
    holder = holder.astype(piece.dtype)
    arrived = lax.all_to_all(holder, "blk", split_axis=0, concat_axis=0, tiled=True)
    take = one_hot(take_from, block_count, piece.dtype)
    routed = jnp.einsum("kj,jrn->krn", take, arrived, preferred_element_type=jnp.float32)
    return routed.astype(piece.dtype)


def local(rhs, inverse, left_factors, right_factors, sources, ranks, owner):
    assert rhs.shape[1] == 1
    level_count = sources.shape[0]
    block_count = owner.shape[1]
    row_count = lax.axis_size("lvl")
    rank_width = left_factors.shape[4]
    rhs_here = rhs[0, 0]
    inverse_here = inverse[0, 0]
    left_here = left_factors[0, 0]
    right_here = right_factors[0, 0]
    my_row = lax.axis_index("lvl")
    me = lax.axis_index("blk")
    tables = routing_tables(sources, owner, ranks)
    mine_src = [None] + [mine(tables[t][0], me) for t in range(1, level_count)]
    mine_rank = [None] + [mine(tables[t][1], me) for t in range(1, level_count)]
    mine_target = [None] + [mine(tables[t][2], me) for t in range(1, level_count)]
    lanes = jnp.arange(rank_width, dtype=jnp.int32)

    def keep_of(t):
        return (lanes[None, :] < mine_rank[t][:, None]).astype(jnp.float32)

    last = level_count - 1
    tile_count, block_rows, _ = left_here.shape
    columns = rhs_here.shape[-1]
    width = columns // row_count
    flat = tile_count * rank_width
    packed = jnp.concatenate(
        [
            inverse_here,
            right_here.transpose(1, 0, 2).reshape(block_rows, flat),
            left_here.transpose(1, 0, 2).reshape(block_rows, flat),
        ],
        axis=1,
    )
    shifted = [packed] + [shift(packed, d, row_count) for d in range(1, row_count)]

    def level_data(t):
        pick = lax.rem(my_row - t + row_count, row_count)
        data = shifted[row_count - 1]
        for d in reversed(range(row_count - 1)):
            data = jnp.where(pick == d, shifted[d], data)
        return (
            data[:, :block_rows],
            data[:, block_rows:block_rows + flat],
            data[:, block_rows + flat:],
        )

    solved = jnp.zeros(rhs_here.shape, jnp.bfloat16)
    incoming = None
    for t in range(level_count):
        current = rhs_here.astype(jnp.float32)
        if t > 0:
            masked = incoming * keep_of(t)[..., None].astype(jnp.bfloat16)
            current = current - jnp.einsum(
                "kbr,krn->bn", left_here, masked, preferred_element_type=jnp.float32
            )
        lowered = current.astype(jnp.bfloat16)
        result = jnp.einsum(
            "ab,bn->an", inverse_here, lowered, preferred_element_type=jnp.float32
        ).astype(jnp.bfloat16)
        solved = jnp.where(my_row == t, result, solved)
        if t + 1 < level_count:
            out = jnp.einsum(
                "kbr,bn->krn", right_here, result, preferred_element_type=jnp.float32
            ).astype(jnp.bfloat16)
            piece = spread(out, t, row_count, my_row)
            routed = route(piece, mine_target[t + 1], mine_src[t + 1], block_count)
            incoming = collect(routed, t + 1, row_count)
        if t == last - 1:
            by_block = solved.reshape(block_rows, row_count, width)
            sent = [by_block[:, 0, :] * 0]
            for d in range(1, row_count):
                wanted = lax.rem(my_row + d, row_count)
                part = jnp.sum(
                    by_block * one_hot_rows(wanted, row_count, by_block.dtype)[None, :, None], axis=1
                ).astype(by_block.dtype)
                sent.append(shift(part, d, row_count))
            own = jnp.sum(
                by_block * one_hot_rows(my_row, row_count, by_block.dtype)[None, :, None], axis=1
            ).astype(by_block.dtype)

    def forward_block(t):
        pick = lax.rem(my_row - t + row_count, row_count)
        block = own
        for d in range(1, row_count):
            block = jnp.where(pick == d, sent[d], block)
        return block

    top = jnp.einsum(
        "ba,bn->an", inverse_here, solved, preferred_element_type=jnp.float32
    ).astype(jnp.bfloat16)
    projected = jnp.einsum("kbr,bn->krn", left_here, top, preferred_element_type=jnp.float32)
    out = (projected * keep_of(last)[..., None]).astype(jnp.bfloat16)
    piece = spread(out, last, row_count, my_row)
    returning = route(piece, mine_src[last], mine_target[last], block_count)
    blocks = [None] * level_count
    for t in reversed(range(last)):
        inverse_t, right_t, left_t = level_data(t)
        current = forward_block(t).astype(jnp.float32) - jnp.dot(
            right_t, returning.reshape(flat, width), preferred_element_type=jnp.float32
        )
        upper = current.astype(jnp.bfloat16)
        result = jnp.einsum(
            "ba,bn->an", inverse_t, upper, preferred_element_type=jnp.float32
        ).astype(jnp.bfloat16)
        blocks[t] = result
        if t > 0:
            projected = jnp.einsum(
                "bm,bn->mn", left_t, result, preferred_element_type=jnp.float32
            ).reshape(tile_count, rank_width, width)
            out = (projected * keep_of(t)[..., None]).astype(jnp.bfloat16)
            returning = route(out, mine_src[t], mine_target[t], block_count)
    mine_blocks = blocks[:last] + [jnp.zeros_like(blocks[0])]
    placed = one_hot_rows(my_row, row_count, jnp.bfloat16)[None, :, None] * blocks_of(mine_blocks, my_row, 0, row_count)[:, None, :]
    for d in range(1, row_count):
        got = shift(blocks_of(mine_blocks, my_row, d, row_count), d, row_count)
        origin = lax.rem(my_row - d + row_count, row_count)
        placed = placed + one_hot_rows(origin, row_count, jnp.bfloat16)[None, :, None] * got[:, None, :]
    answer = jnp.where(my_row == last, top, placed.reshape(block_rows, columns))
    return (solved[None, None], answer[None, None])


def solution(mesh):
    return jax.shard_map(
        local,
        mesh=mesh,
        in_specs=(
            P("lvl", "blk", None, None),
            P("lvl", "blk", None, None),
            P("lvl", "blk", None, None, None),
            P("lvl", "blk", None, None, None),
            P(),
            P(),
            P(),
        ),
        out_specs=(P("lvl", "blk", None, None), P("lvl", "blk", None, None)),
        check_vma=False,
    )
```

```python
import jax
import jax.numpy as jnp
from jax import lax
from jax.sharding import PartitionSpec as P


def routing_tables(sources, owner, ranks):
    level_count, block_count = owner.shape
    position = jnp.arange(block_count, dtype=jnp.int32)
    tables = [None]
    for t in range(1, level_count):
        at_pos = (owner[t][None, :] == position[:, None]).astype(jnp.int32)
        src_block = jnp.sum(at_pos[:, :, None] * sources[t][None, :, :], axis=1)
        rank_pos = jnp.sum(at_pos[:, :, None] * ranks[t][None, :, :], axis=1)
        pick = (src_block[:, :, None] == position[None, None, :]).astype(jnp.int32)
        src_pos = jnp.sum(pick * owner[t - 1][None, None, :], axis=2)
        hit = (src_pos[:, None, :] == position[None, :, None]).astype(jnp.int32)
        target_of = jnp.sum(hit * position[:, None, None], axis=0)
        tables.append((src_pos, rank_pos, target_of))
    return tables


def mine(table, me):
    block_count = table.shape[0]
    row = (jnp.arange(block_count, dtype=jnp.int32) == me).astype(jnp.int32)
    return jnp.sum(row[:, None] * table, axis=0)


def one_hot(index, count, dtype):
    return (index[:, None] == jnp.arange(count, dtype=jnp.int32)[None, :]).astype(dtype)


def spread(out, src_row, row_count, my_row):
    width = out.shape[-1] // row_count
    piece = None
    for r in range(row_count):
        part = out[..., r * width:(r + 1) * width]
        if r == src_row:
            got = jnp.where(my_row == r, part, jnp.zeros_like(part))
        else:
            got = lax.ppermute(part, "lvl", [(src_row, r)])
        piece = got if piece is None else piece + got
    return piece


def collect(routed, dst_row, row_count):
    parts = []
    for r in range(row_count):
        if r == dst_row:
            parts.append(routed)
        else:
            parts.append(lax.ppermute(routed, "lvl", [(r, dst_row)]))
    return jnp.concatenate(parts, axis=-1)


def shift(array, by, row_count):
    return lax.ppermute(array, "lvl", [(i, (i + by) % row_count) for i in range(row_count)])


def one_hot_rows(index, count, dtype):
    return (jnp.arange(count, dtype=jnp.int32) == index).astype(dtype)


def blocks_of(level_blocks, my_row, by, row_count):
    wanted = lax.rem(my_row + by, row_count)
    chosen = level_blocks[0]
    for t in range(1, len(level_blocks)):
        chosen = jnp.where(wanted == t, level_blocks[t], chosen)
    return chosen


def route(piece, send_to, take_from, block_count):
    send = one_hot(send_to, block_count, piece.dtype)
    holder = jnp.einsum("kj,krn->jrn", send, piece, preferred_element_type=jnp.float32)
    holder = holder.astype(piece.dtype)
    arrived = lax.all_to_all(holder, "blk", split_axis=0, concat_axis=0, tiled=True)
    take = one_hot(take_from, block_count, piece.dtype)
    routed = jnp.einsum("kj,jrn->krn", take, arrived, preferred_element_type=jnp.float32)
    return routed.astype(piece.dtype)


def local(rhs, inverse, left_factors, right_factors, sources, ranks, owner):
    assert rhs.shape[1] == 1
    level_count = sources.shape[0]
    block_count = owner.shape[1]
    row_count = lax.axis_size("lvl")
    rank_width = left_factors.shape[4]
    rhs_here = rhs[0, 0]
    inverse_here = inverse[0, 0]
    left_here = left_factors[0, 0]
    right_here = right_factors[0, 0]
    my_row = lax.axis_index("lvl")
    me = lax.axis_index("blk")
    tables = routing_tables(sources, owner, ranks)
    mine_src = [None] + [mine(tables[t][0], me) for t in range(1, level_count)]
    mine_rank = [None] + [mine(tables[t][1], me) for t in range(1, level_count)]
    mine_target = [None] + [mine(tables[t][2], me) for t in range(1, level_count)]
    lanes = jnp.arange(rank_width, dtype=jnp.int32)

    def keep_of(t):
        return (lanes[None, :] < mine_rank[t][:, None]).astype(jnp.float32)

    last = level_count - 1
    tile_count, block_rows, _ = left_here.shape
    columns = rhs_here.shape[-1]
    width = columns // row_count
    flat = tile_count * rank_width
    packed = jnp.concatenate(
        [
            inverse_here,
            right_here.transpose(1, 0, 2).reshape(block_rows, flat),
            left_here.transpose(1, 0, 2).reshape(block_rows, flat),
        ],
        axis=1,
    )
    gathered = lax.all_gather(packed, "lvl")

    def level_data(t):
        data = gathered[t]
        return (
            data[:, :block_rows],
            data[:, block_rows:block_rows + flat],
            data[:, block_rows + flat:],
        )

    solved = jnp.zeros(rhs_here.shape, jnp.bfloat16)
    incoming = None
    for t in range(level_count):
        current = rhs_here.astype(jnp.float32)
        if t > 0:
            masked = incoming * keep_of(t)[..., None].astype(jnp.bfloat16)
            current = current - jnp.einsum(
                "kbr,krn->bn", left_here, masked, preferred_element_type=jnp.float32
            )
        lowered = current.astype(jnp.bfloat16)
        result = jnp.einsum(
            "ab,bn->an", inverse_here, lowered, preferred_element_type=jnp.float32
        ).astype(jnp.bfloat16)
        solved = jnp.where(my_row == t, result, solved)
        if t + 1 < level_count:
            out = jnp.einsum(
                "kbr,bn->krn", right_here, result, preferred_element_type=jnp.float32
            ).astype(jnp.bfloat16)
            piece = spread(out, t, row_count, my_row)
            routed = route(piece, mine_target[t + 1], mine_src[t + 1], block_count)
            incoming = collect(routed, t + 1, row_count)
        if t == last - 1:
            forward_all = lax.all_gather(solved, "lvl")

    def forward_block(t):
        by_block = forward_all[t].reshape(block_rows, row_count, width)
        return jnp.sum(
            by_block * one_hot_rows(my_row, row_count, by_block.dtype)[None, :, None], axis=1
        ).astype(by_block.dtype)

    top = jnp.einsum(
        "ba,bn->an", inverse_here, solved, preferred_element_type=jnp.float32
    ).astype(jnp.bfloat16)
    projected = jnp.einsum("kbr,bn->krn", left_here, top, preferred_element_type=jnp.float32)
    out = (projected * keep_of(last)[..., None]).astype(jnp.bfloat16)
    piece = spread(out, last, row_count, my_row)
    returning = route(piece, mine_src[last], mine_target[last], block_count)
    blocks = [None] * level_count
    for t in reversed(range(last)):
        inverse_t, right_t, left_t = level_data(t)
        current = forward_block(t).astype(jnp.float32) - jnp.dot(
            right_t, returning.reshape(flat, width), preferred_element_type=jnp.float32
        )
        upper = current.astype(jnp.bfloat16)
        result = jnp.einsum(
            "ba,bn->an", inverse_t, upper, preferred_element_type=jnp.float32
        ).astype(jnp.bfloat16)
        blocks[t] = result
        if t > 0:
            projected = jnp.einsum(
                "bm,bn->mn", left_t, result, preferred_element_type=jnp.float32
            ).reshape(tile_count, rank_width, width)
            out = (projected * keep_of(t)[..., None]).astype(jnp.bfloat16)
            returning = route(out, mine_src[t], mine_target[t], block_count)
    mine_blocks = blocks[:last] + [jnp.zeros_like(blocks[0])]
    placed = one_hot_rows(my_row, row_count, jnp.bfloat16)[None, :, None] * blocks_of(mine_blocks, my_row, 0, row_count)[:, None, :]
    for d in range(1, row_count):
        got = shift(blocks_of(mine_blocks, my_row, d, row_count), d, row_count)
        origin = lax.rem(my_row - d + row_count, row_count)
        placed = placed + one_hot_rows(origin, row_count, jnp.bfloat16)[None, :, None] * got[:, None, :]
    answer = jnp.where(my_row == last, top, placed.reshape(block_rows, columns))
    return (solved[None, None], answer[None, None])


def solution(mesh):
    return jax.shard_map(
        local,
        mesh=mesh,
        in_specs=(
            P("lvl", "blk", None, None),
            P("lvl", "blk", None, None),
            P("lvl", "blk", None, None, None),
            P("lvl", "blk", None, None, None),
            P(),
            P(),
            P(),
        ),
        out_specs=(P("lvl", "blk", None, None), P("lvl", "blk", None, None)),
        check_vma=False,
    )
```

```python
import jax
import jax.numpy as jnp
from jax import lax
from jax.sharding import PartitionSpec as P


def routing_tables(sources, owner, ranks):
    level_count, block_count = owner.shape
    position = jnp.arange(block_count, dtype=jnp.int32)
    tables = [None]
    for t in range(1, level_count):
        at_pos = (owner[t][None, :] == position[:, None]).astype(jnp.int32)
        src_block = jnp.sum(at_pos[:, :, None] * sources[t][None, :, :], axis=1)
        rank_pos = jnp.sum(at_pos[:, :, None] * ranks[t][None, :, :], axis=1)
        pick = (src_block[:, :, None] == position[None, None, :]).astype(jnp.int32)
        src_pos = jnp.sum(pick * owner[t - 1][None, None, :], axis=2)
        hit = (src_pos[:, None, :] == position[None, :, None]).astype(jnp.int32)
        target_of = jnp.sum(hit * position[:, None, None], axis=0)
        tables.append((src_pos, rank_pos, target_of))
    return tables


def mine(table, me):
    block_count = table.shape[0]
    row = (jnp.arange(block_count, dtype=jnp.int32) == me).astype(jnp.int32)
    return jnp.sum(row[:, None] * table, axis=0)


def one_hot(index, count, dtype):
    return (index[:, None] == jnp.arange(count, dtype=jnp.int32)[None, :]).astype(dtype)


def spread(out, src_row, row_count, my_row):
    width = out.shape[-1] // row_count
    piece = None
    for r in range(row_count):
        part = out[..., r * width:(r + 1) * width]
        if r == src_row:
            got = jnp.where(my_row == r, part, jnp.zeros_like(part))
        else:
            got = lax.ppermute(part, "lvl", [(src_row, r)])
        piece = got if piece is None else piece + got
    return piece


def collect(routed, dst_row, row_count):
    parts = []
    for r in range(row_count):
        if r == dst_row:
            parts.append(routed)
        else:
            parts.append(lax.ppermute(routed, "lvl", [(r, dst_row)]))
    return jnp.concatenate(parts, axis=-1)


def shift(array, by, row_count):
    return lax.ppermute(array, "lvl", [(i, (i + by) % row_count) for i in range(row_count)])


def one_hot_rows(index, count, dtype):
    return (jnp.arange(count, dtype=jnp.int32) == index).astype(dtype)


def blocks_of(level_blocks, my_row, by, row_count):
    wanted = lax.rem(my_row + by, row_count)
    chosen = level_blocks[0]
    for t in range(1, len(level_blocks)):
        chosen = jnp.where(wanted == t, level_blocks[t], chosen)
    return chosen


def route(piece, send_to, take_from, block_count):
    send = one_hot(send_to, block_count, piece.dtype)
    holder = jnp.einsum("kj,krn->jrn", send, piece, preferred_element_type=jnp.float32)
    holder = holder.astype(piece.dtype)
    arrived = lax.all_to_all(holder, "blk", split_axis=0, concat_axis=0, tiled=True)
    take = one_hot(take_from, block_count, piece.dtype)
    routed = jnp.einsum("kj,jrn->krn", take, arrived, preferred_element_type=jnp.float32)
    return routed.astype(piece.dtype)


def local(rhs, inverse, left_factors, right_factors, sources, ranks, owner):
    assert rhs.shape[1] == 1
    level_count = sources.shape[0]
    block_count = owner.shape[1]
    row_count = lax.axis_size("lvl")
    rank_width = left_factors.shape[4]
    rhs_here = rhs[0, 0]
    inverse_here = inverse[0, 0]
    left_here = left_factors[0, 0]
    right_here = right_factors[0, 0]
    my_row = lax.axis_index("lvl")
    me = lax.axis_index("blk")
    tables = routing_tables(sources, owner, ranks)
    mine_src = [None] + [mine(tables[t][0], me) for t in range(1, level_count)]
    mine_rank = [None] + [mine(tables[t][1], me) for t in range(1, level_count)]
    mine_target = [None] + [mine(tables[t][2], me) for t in range(1, level_count)]
    lanes = jnp.arange(rank_width, dtype=jnp.int32)

    def keep_of(t):
        return (lanes[None, :] < mine_rank[t][:, None]).astype(jnp.float32)

    last = level_count - 1
    tile_count, block_rows, _ = left_here.shape
    columns = rhs_here.shape[-1]
    width = columns // row_count
    flat = tile_count * rank_width
    packed = jnp.concatenate(
        [
            inverse_here,
            right_here.transpose(1, 0, 2).reshape(block_rows, flat),
            left_here.transpose(1, 0, 2).reshape(block_rows, flat),
        ],
        axis=1,
    )
    gathered = lax.all_gather(packed, "lvl")

    def level_data(t):
        data = gathered[t]
        return (
            data[:, :block_rows],
            data[:, block_rows:block_rows + flat],
            data[:, block_rows + flat:],
        )

    solved = jnp.zeros(rhs_here.shape, jnp.bfloat16)
    incoming = None
    for t in range(level_count):
        current = rhs_here.astype(jnp.float32)
        if t > 0:
            masked = incoming * keep_of(t)[..., None].astype(jnp.bfloat16)
            current = current - jnp.einsum(
                "kbr,krn->bn", left_here, masked, preferred_element_type=jnp.float32
            )
        lowered = current.astype(jnp.bfloat16)
        result = jnp.einsum(
            "ab,bn->an", inverse_here, lowered, preferred_element_type=jnp.float32
        ).astype(jnp.bfloat16)
        solved = jnp.where(my_row == t, result, solved)
        if t + 1 < level_count:
            out = jnp.einsum(
                "kbr,bn->krn", right_here, result, preferred_element_type=jnp.float32
            ).astype(jnp.bfloat16)
            piece = spread(out, t, row_count, my_row)
            routed = route(piece, mine_target[t + 1], mine_src[t + 1], block_count)
            incoming = collect(routed, t + 1, row_count)
        if t == last - 1:
            by_block = solved.reshape(block_rows, row_count, width)
            sent = [None]
            for d in range(1, row_count):
                wanted = lax.rem(my_row + d, row_count)
                part = jnp.sum(
                    by_block * one_hot_rows(wanted, row_count, by_block.dtype)[None, :, None], axis=1
                ).astype(by_block.dtype)
                sent.append(shift(part, d, row_count))
            own = jnp.sum(
                by_block * one_hot_rows(my_row, row_count, by_block.dtype)[None, :, None], axis=1
            ).astype(by_block.dtype)

    def forward_block(t):
        pick = lax.rem(my_row - t + row_count, row_count)
        block = own
        for d in range(1, row_count):
            block = jnp.where(pick == d, sent[d], block)
        return block

    top = jnp.einsum(
        "ba,bn->an", inverse_here, solved, preferred_element_type=jnp.float32
    ).astype(jnp.bfloat16)
    projected = jnp.einsum("kbr,bn->krn", left_here, top, preferred_element_type=jnp.float32)
    out = (projected * keep_of(last)[..., None]).astype(jnp.bfloat16)
    piece = spread(out, last, row_count, my_row)
    returning = route(piece, mine_src[last], mine_target[last], block_count)
    blocks = [None] * level_count
    for t in reversed(range(last)):
        inverse_t, right_t, left_t = level_data(t)
        current = forward_block(t).astype(jnp.float32) - jnp.dot(
            right_t, returning.reshape(flat, width), preferred_element_type=jnp.float32
        )
        upper = current.astype(jnp.bfloat16)
        result = jnp.einsum(
            "ba,bn->an", inverse_t, upper, preferred_element_type=jnp.float32
        ).astype(jnp.bfloat16)
        blocks[t] = result
        if t > 0:
            projected = jnp.einsum(
                "bm,bn->mn", left_t, result, preferred_element_type=jnp.float32
            ).reshape(tile_count, rank_width, width)
            out = (projected * keep_of(t)[..., None]).astype(jnp.bfloat16)
            returning = route(out, mine_src[t], mine_target[t], block_count)
    mine_blocks = blocks[:last] + [jnp.zeros_like(blocks[0])]
    placed = one_hot_rows(my_row, row_count, jnp.bfloat16)[None, :, None] * blocks_of(mine_blocks, my_row, 0, row_count)[:, None, :]
    for d in range(1, row_count):
        got = shift(blocks_of(mine_blocks, my_row, d, row_count), d, row_count)
        origin = lax.rem(my_row - d + row_count, row_count)
        placed = placed + one_hot_rows(origin, row_count, jnp.bfloat16)[None, :, None] * got[:, None, :]
    answer = jnp.where(my_row == last, top, placed.reshape(block_rows, columns))
    return (solved[None, None], answer[None, None])


def solution(mesh):
    return jax.shard_map(
        local,
        mesh=mesh,
        in_specs=(
            P("lvl", "blk", None, None),
            P("lvl", "blk", None, None),
            P("lvl", "blk", None, None, None),
            P("lvl", "blk", None, None, None),
            P(),
            P(),
            P(),
        ),
        out_specs=(P("lvl", "blk", None, None), P("lvl", "blk", None, None)),
        check_vma=False,
    )
```

```python
import jax
import jax.numpy as jnp
from jax import lax
from jax.sharding import PartitionSpec as P


def routing_tables(sources, owner, ranks):
    level_count, block_count = owner.shape
    position = jnp.arange(block_count, dtype=jnp.int32)
    tables = [None]
    for t in range(1, level_count):
        at_pos = (owner[t][None, :] == position[:, None]).astype(jnp.int32)
        src_block = jnp.sum(at_pos[:, :, None] * sources[t][None, :, :], axis=1)
        rank_pos = jnp.sum(at_pos[:, :, None] * ranks[t][None, :, :], axis=1)
        pick = (src_block[:, :, None] == position[None, None, :]).astype(jnp.int32)
        src_pos = jnp.sum(pick * owner[t - 1][None, None, :], axis=2)
        hit = (src_pos[:, None, :] == position[None, :, None]).astype(jnp.int32)
        target_of = jnp.sum(hit * position[:, None, None], axis=0)
        tables.append((src_pos, rank_pos, target_of))
    return tables


def mine(table, me):
    block_count = table.shape[0]
    row = (jnp.arange(block_count, dtype=jnp.int32) == me).astype(jnp.int32)
    return jnp.sum(row[:, None] * table, axis=0)


def one_hot(index, count, dtype):
    return (index[:, None] == jnp.arange(count, dtype=jnp.int32)[None, :]).astype(dtype)


def spread(out, src_row, row_count, my_row):
    width = out.shape[-1] // row_count
    piece = None
    for r in range(row_count):
        part = out[..., r * width:(r + 1) * width]
        if r == src_row:
            got = jnp.where(my_row == r, part, jnp.zeros_like(part))
        else:
            got = lax.ppermute(part, "lvl", [(src_row, r)])
        piece = got if piece is None else piece + got
    return piece


def collect(routed, dst_row, row_count):
    parts = []
    for r in range(row_count):
        if r == dst_row:
            parts.append(routed)
        else:
            parts.append(lax.ppermute(routed, "lvl", [(r, dst_row)]))
    return jnp.concatenate(parts, axis=-1)


def shift(array, by, row_count):
    return lax.ppermute(array, "lvl", [(i, (i + by) % row_count) for i in range(row_count)])


def one_hot_rows(index, count, dtype):
    return (jnp.arange(count, dtype=jnp.int32) == index).astype(dtype)


def blocks_of(level_blocks, my_row, by, row_count):
    wanted = lax.rem(my_row + by, row_count)
    chosen = level_blocks[0]
    for t in range(1, len(level_blocks)):
        chosen = jnp.where(wanted == t, level_blocks[t], chosen)
    return chosen


def pick_block(blocks, index, count):
    hot = (jnp.arange(count, dtype=jnp.int32) == index).astype(blocks.dtype)
    return jnp.sum(blocks * hot[None, :, None], axis=1).astype(blocks.dtype)


def frees_at(parts, my_row, t, row_count):
    pick = lax.rem(my_row - t + row_count, row_count)
    chosen = parts[0]
    for d in range(1, row_count):
        chosen = jnp.where(pick == d, parts[d], chosen)
    return chosen


def route(piece, send_to, take_from, block_count):
    send = one_hot(send_to, block_count, piece.dtype)
    holder = jnp.einsum("kj,krn->jrn", send, piece, preferred_element_type=jnp.float32)
    holder = holder.astype(piece.dtype)
    arrived = lax.all_to_all(holder, "blk", split_axis=0, concat_axis=0, tiled=True)
    take = one_hot(take_from, block_count, piece.dtype)
    routed = jnp.einsum("kj,jrn->krn", take, arrived, preferred_element_type=jnp.float32)
    return routed.astype(piece.dtype)


def local(rhs, inverse, left_factors, right_factors, sources, ranks, owner):
    assert rhs.shape[1] == 1
    level_count = sources.shape[0]
    block_count = owner.shape[1]
    row_count = lax.axis_size("lvl")
    rank_width = left_factors.shape[4]
    rhs_here = rhs[0, 0]
    inverse_here = inverse[0, 0]
    left_here = left_factors[0, 0]
    right_here = right_factors[0, 0]
    my_row = lax.axis_index("lvl")
    me = lax.axis_index("blk")
    tables = routing_tables(sources, owner, ranks)
    mine_src = [None] + [mine(tables[t][0], me) for t in range(1, level_count)]
    mine_rank = [None] + [mine(tables[t][1], me) for t in range(1, level_count)]
    mine_target = [None] + [mine(tables[t][2], me) for t in range(1, level_count)]
    lanes = jnp.arange(rank_width, dtype=jnp.int32)

    def keep_of(t):
        return (lanes[None, :] < mine_rank[t][:, None]).astype(jnp.float32)

    last = level_count - 1
    tile_count, block_rows, _ = left_here.shape
    columns = rhs_here.shape[-1]
    width = columns // row_count
    flat = tile_count * rank_width
    my_rank = jnp.zeros((tile_count,), jnp.int32)
    for t in range(1, level_count):
        my_rank = jnp.where(my_row == t, mine_rank[t], my_rank)
    keep = (lanes[None, :] < my_rank[:, None]).astype(left_here.dtype)
    left_flat = (left_here * keep[:, None, :]).transpose(1, 0, 2).reshape(block_rows, flat)
    right_flat = right_here.transpose(1, 0, 2).reshape(block_rows, flat)

    def dot(a, b, spec):
        return jnp.einsum(spec, a, b, preferred_element_type=jnp.float32)

    inv_left = dot(inverse_here, left_flat, "ab,bm->am").astype(jnp.bfloat16)
    couple = dot(right_flat, inv_left, "bq,bm->qm").astype(jnp.bfloat16)
    inv_rhs = dot(inverse_here, rhs_here, "ab,bn->an").astype(jnp.bfloat16)
    free = dot(right_flat, inv_rhs, "bq,bn->qn").astype(jnp.bfloat16)
    couples = [couple] + [shift(couple, d, row_count) for d in range(1, row_count)]
    free_blocks = free.reshape(flat, row_count, width)
    frees = [pick_block(free_blocks, my_row, row_count)]
    for d in range(1, row_count):
        frees.append(shift(pick_block(free_blocks, lax.rem(my_row + d, row_count), row_count), d, row_count))

    def from_row(parts, t):
        pick = lax.rem(my_row - t + row_count, row_count)
        chosen = parts[row_count - 1]
        for d in reversed(range(row_count - 1)):
            chosen = jnp.where(pick == d, parts[d], chosen)
        return chosen

    def solve_forward(coef_full):
        lower = rhs_here.astype(jnp.float32) - dot(
            left_flat, coef_full.reshape(flat, columns), "bm,mn->bn"
        )
        return dot(inverse_here, lower.astype(jnp.bfloat16), "ab,bn->an").astype(jnp.bfloat16)

    def solve_backward(fwd, back_full):
        upper = fwd.astype(jnp.float32) - dot(
            right_flat, back_full.reshape(flat, columns), "bm,mn->bn"
        )
        return dot(inverse_here, upper.astype(jnp.bfloat16), "ba,bn->an").astype(jnp.bfloat16)

    lane_shape = (tile_count, rank_width, width)
    first = dot(inverse_here, rhs_here, "ab,bn->an").astype(jnp.bfloat16)
    out = dot(right_flat, first, "bq,bn->qn").astype(jnp.bfloat16)
    piece = spread(out.reshape(tile_count, rank_width, columns), 0, row_count, my_row)
    chain = [None] * level_count
    chain[1] = route(piece, mine_target[1], mine_src[1], block_count)
    couple_at = [None] + [from_row(couples, t) for t in range(1, last)]
    for t in range(1, last):
        step = frees_at(frees, my_row, t, row_count).astype(jnp.float32) - dot(
            couple_at[t], chain[t].reshape(flat, width), "qm,mn->qn"
        )
        chain[t + 1] = route(step.astype(jnp.bfloat16).reshape(lane_shape), mine_target[t + 1], mine_src[t + 1], block_count)

    solved = jnp.where(my_row == 0, first, jnp.zeros_like(first))
    back_free = [None] * level_count
    for t in range(1, last):
        coef_full = collect(chain[t], t, row_count)

        def owner(coef_full):
            fwd = solve_forward(coef_full)
            back_in = dot(inverse_here, fwd, "ba,bn->an").astype(jnp.bfloat16)
            return fwd, dot(left_flat, back_in, "bm,bn->mn").astype(jnp.bfloat16)

        def other(coef_full):
            return jnp.zeros_like(rhs_here), jnp.zeros((flat, columns), jnp.bfloat16)

        fwd, back_term = lax.cond(my_row == t, owner, other, coef_full)
        solved = jnp.where(my_row == t, fwd, solved)
        back_free[t] = spread(back_term.reshape(tile_count, rank_width, columns), t, row_count, my_row)

    top_fwd = solve_forward(collect(chain[last], last, row_count))
    solved = jnp.where(my_row == last, top_fwd, solved)
    top = dot(inverse_here, top_fwd, "ba,bn->an").astype(jnp.bfloat16)
    out = dot(left_flat, top, "bm,bn->mn").astype(jnp.bfloat16)
    piece = spread(out.reshape(tile_count, rank_width, columns), last, row_count, my_row)
    back = [None] * level_count
    back[last - 1] = route(piece, mine_src[last], mine_target[last], block_count)
    for t in reversed(range(1, last)):
        step = back_free[t].reshape(flat, width).astype(jnp.float32) - dot(
            couple_at[t], back[t].reshape(flat, width), "mq,mn->qn"
        )
        back[t - 1] = route(step.astype(jnp.bfloat16).reshape(lane_shape), mine_src[t], mine_target[t], block_count)

    answer = jnp.where(my_row == last, top, jnp.zeros_like(top))
    for t in reversed(range(last)):
        back_full = collect(back[t], t, row_count)
        if t > 0:
            result = lax.cond(
                my_row == t,
                lambda ops: solve_backward(*ops),
                lambda ops: jnp.zeros_like(rhs_here),
                (solved, back_full),
            )
        else:
            result = solve_backward(solved, back_full)
        answer = jnp.where(my_row == t, result, answer)
    return (solved[None, None], answer[None, None])


def solution(mesh):
    return jax.shard_map(
        local,
        mesh=mesh,
        in_specs=(
            P("lvl", "blk", None, None),
            P("lvl", "blk", None, None),
            P("lvl", "blk", None, None, None),
            P("lvl", "blk", None, None, None),
            P(),
            P(),
            P(),
        ),
        out_specs=(P("lvl", "blk", None, None), P("lvl", "blk", None, None)),
        check_vma=False,
    )
```

```python
import jax
import jax.numpy as jnp
from jax import lax
from jax.sharding import PartitionSpec as P


def routing_tables(sources, owner, ranks):
    level_count, block_count = owner.shape
    position = jnp.arange(block_count, dtype=jnp.int32)
    tables = [None]
    for t in range(1, level_count):
        at_pos = (owner[t][None, :] == position[:, None]).astype(jnp.int32)
        src_block = jnp.sum(at_pos[:, :, None] * sources[t][None, :, :], axis=1)
        rank_pos = jnp.sum(at_pos[:, :, None] * ranks[t][None, :, :], axis=1)
        pick = (src_block[:, :, None] == position[None, None, :]).astype(jnp.int32)
        src_pos = jnp.sum(pick * owner[t - 1][None, None, :], axis=2)
        hit = (src_pos[:, None, :] == position[None, :, None]).astype(jnp.int32)
        target_of = jnp.sum(hit * position[:, None, None], axis=0)
        tables.append((src_pos, rank_pos, target_of))
    return tables


def mine(table, me):
    block_count = table.shape[0]
    row = (jnp.arange(block_count, dtype=jnp.int32) == me).astype(jnp.int32)
    return jnp.sum(row[:, None] * table, axis=0)


def one_hot(index, count, dtype):
    return (index[:, None] == jnp.arange(count, dtype=jnp.int32)[None, :]).astype(dtype)


def spread(out, src_row, row_count, my_row):
    width = out.shape[-1] // row_count
    piece = None
    for r in range(row_count):
        part = out[..., r * width:(r + 1) * width]
        if r == src_row:
            got = jnp.where(my_row == r, part, jnp.zeros_like(part))
        else:
            got = lax.ppermute(part, "lvl", [(src_row, r)])
        piece = got if piece is None else piece + got
    return piece


def collect(routed, dst_row, row_count):
    parts = []
    for r in range(row_count):
        if r == dst_row:
            parts.append(routed)
        else:
            parts.append(lax.ppermute(routed, "lvl", [(r, dst_row)]))
    return jnp.concatenate(parts, axis=-1)


def shift(array, by, row_count):
    return lax.ppermute(array, "lvl", [(i, (i + by) % row_count) for i in range(row_count)])


def one_hot_rows(index, count, dtype):
    return (jnp.arange(count, dtype=jnp.int32) == index).astype(dtype)


def blocks_of(level_blocks, my_row, by, row_count):
    wanted = lax.rem(my_row + by, row_count)
    chosen = level_blocks[0]
    for t in range(1, len(level_blocks)):
        chosen = jnp.where(wanted == t, level_blocks[t], chosen)
    return chosen


def of_level(parts, index):
    chosen = parts[0]
    for t in range(1, len(parts)):
        chosen = jnp.where(index == t, parts[t], chosen)
    return chosen


def take_block(full, index, count):
    width = full.shape[-1] // count
    blocks = full.reshape(full.shape[:-1] + (count, width))
    hot = (jnp.arange(count, dtype=jnp.int32) == index).astype(full.dtype)
    return jnp.sum(blocks * hot[:, None], axis=-2).astype(full.dtype)


def put_block(part, index, count):
    hot = (jnp.arange(count, dtype=jnp.int32) == index).astype(part.dtype)
    full = part[..., None, :] * hot[:, None]
    return full.reshape(part.shape[:-1] + (count * part.shape[-1],))


def pick_block(blocks, index, count):
    hot = (jnp.arange(count, dtype=jnp.int32) == index).astype(blocks.dtype)
    return jnp.sum(blocks * hot[None, :, None], axis=1).astype(blocks.dtype)


def frees_at(parts, my_row, t, row_count):
    pick = lax.rem(my_row - t + row_count, row_count)
    chosen = parts[0]
    for d in range(1, row_count):
        chosen = jnp.where(pick == d, parts[d], chosen)
    return chosen


def route(piece, send_to, take_from, block_count):
    send = one_hot(send_to, block_count, piece.dtype)
    holder = jnp.einsum("kj,krn->jrn", send, piece, preferred_element_type=jnp.float32)
    holder = holder.astype(piece.dtype)
    arrived = lax.all_to_all(holder, "blk", split_axis=0, concat_axis=0, tiled=True)
    take = one_hot(take_from, block_count, piece.dtype)
    routed = jnp.einsum("kj,jrn->krn", take, arrived, preferred_element_type=jnp.float32)
    return routed.astype(piece.dtype)


def local(rhs, inverse, left_factors, right_factors, sources, ranks, owner):
    assert rhs.shape[1] == 1
    level_count = sources.shape[0]
    block_count = owner.shape[1]
    row_count = lax.axis_size("lvl")
    rank_width = left_factors.shape[4]
    rhs_here = rhs[0, 0]
    inverse_here = inverse[0, 0]
    left_here = left_factors[0, 0]
    right_here = right_factors[0, 0]
    my_row = lax.axis_index("lvl")
    me = lax.axis_index("blk")
    tables = routing_tables(sources, owner, ranks)
    mine_src = [None] + [mine(tables[t][0], me) for t in range(1, level_count)]
    mine_rank = [None] + [mine(tables[t][1], me) for t in range(1, level_count)]
    mine_target = [None] + [mine(tables[t][2], me) for t in range(1, level_count)]
    lanes = jnp.arange(rank_width, dtype=jnp.int32)

    def keep_of(t):
        return (lanes[None, :] < mine_rank[t][:, None]).astype(jnp.float32)

    last = level_count - 1
    tile_count, block_rows, _ = left_here.shape
    columns = rhs_here.shape[-1]
    width = columns // row_count
    flat = tile_count * rank_width
    my_rank = jnp.zeros((tile_count,), jnp.int32)
    for t in range(1, level_count):
        my_rank = jnp.where(my_row == t, mine_rank[t], my_rank)
    keep = (lanes[None, :] < my_rank[:, None]).astype(left_here.dtype)
    left_flat = (left_here * keep[:, None, :]).transpose(1, 0, 2).reshape(block_rows, flat)
    right_flat = right_here.transpose(1, 0, 2).reshape(block_rows, flat)

    def dot(a, b, spec):
        return jnp.einsum(spec, a, b, preferred_element_type=jnp.float32)

    inv_left = dot(inverse_here, left_flat, "ab,bm->am").astype(jnp.bfloat16)
    couple = dot(right_flat, inv_left, "bq,bm->qm").astype(jnp.bfloat16)
    inv_rhs = dot(inverse_here, rhs_here, "ab,bn->an").astype(jnp.bfloat16)
    free = dot(right_flat, inv_rhs, "bq,bn->qn").astype(jnp.bfloat16)
    couples = [couple] + [shift(couple, d, row_count) for d in range(1, row_count)]
    free_blocks = free.reshape(flat, row_count, width)
    frees = [pick_block(free_blocks, my_row, row_count)]
    for d in range(1, row_count):
        frees.append(shift(pick_block(free_blocks, lax.rem(my_row + d, row_count), row_count), d, row_count))

    def from_row(parts, t):
        pick = lax.rem(my_row - t + row_count, row_count)
        chosen = parts[row_count - 1]
        for d in reversed(range(row_count - 1)):
            chosen = jnp.where(pick == d, parts[d], chosen)
        return chosen

    def solve_forward(coef_full):
        lower = rhs_here.astype(jnp.float32) - dot(
            left_flat, coef_full.reshape(flat, columns), "bm,mn->bn"
        )
        return dot(inverse_here, lower.astype(jnp.bfloat16), "ab,bn->an").astype(jnp.bfloat16)

    def solve_backward(fwd, back_full):
        upper = fwd.astype(jnp.float32) - dot(
            right_flat, back_full.reshape(flat, columns), "bm,mn->bn"
        )
        return dot(inverse_here, upper.astype(jnp.bfloat16), "ba,bn->an").astype(jnp.bfloat16)

    lane_shape = (tile_count, rank_width, width)
    zero_block = jnp.zeros(lane_shape, jnp.bfloat16)

    def own_level_blocks(parts):
        full = put_block(of_level(parts, my_row), my_row, row_count)
        for d in range(1, row_count):
            got = shift(of_level(parts, lax.rem(my_row + d, row_count)), d, row_count)
            full = full + put_block(got, lax.rem(my_row - d + row_count, row_count), row_count)
        return full

    first = dot(inverse_here, rhs_here, "ab,bn->an").astype(jnp.bfloat16)
    out = dot(right_flat, first, "bq,bn->qn").astype(jnp.bfloat16)
    piece = spread(out.reshape(tile_count, rank_width, columns), 0, row_count, my_row)
    chain = [zero_block] * level_count
    chain[1] = route(piece, mine_target[1], mine_src[1], block_count)
    couple_at = [None] + [from_row(couples, t) for t in range(1, last)]
    for t in range(1, last):
        step = frees_at(frees, my_row, t, row_count).astype(jnp.float32) - dot(
            couple_at[t], chain[t].reshape(flat, width), "qm,mn->qn"
        )
        chain[t + 1] = route(step.astype(jnp.bfloat16).reshape(lane_shape), mine_target[t + 1], mine_src[t + 1], block_count)

    mine_fwd = solve_forward(own_level_blocks(chain))
    solved = jnp.where(my_row == 0, first, mine_fwd)
    top = dot(inverse_here, solved, "ba,bn->an").astype(jnp.bfloat16)
    back_term = dot(left_flat, top, "bm,bn->mn").astype(jnp.bfloat16)
    back_parts = [take_block(back_term, my_row, row_count)]
    for d in range(1, row_count):
        back_parts.append(shift(take_block(back_term, lax.rem(my_row + d, row_count), row_count), d, row_count))

    def back_free(t):
        return frees_at(back_parts, my_row, t, row_count)

    back = [zero_block] * level_count
    back[last - 1] = route(back_free(last).reshape(lane_shape), mine_src[last], mine_target[last], block_count)
    for t in reversed(range(1, last)):
        step = back_free(t).astype(jnp.float32) - dot(
            couple_at[t], back[t - 0].reshape(flat, width), "mq,mn->qn"
        )
        back[t - 1] = route(step.astype(jnp.bfloat16).reshape(lane_shape), mine_src[t], mine_target[t], block_count)

    mine_back = solve_backward(solved, own_level_blocks(back[:last] + [zero_block]))
    answer = jnp.where(my_row == last, top, mine_back)
    return (solved[None, None], answer[None, None])


def solution(mesh):
    return jax.shard_map(
        local,
        mesh=mesh,
        in_specs=(
            P("lvl", "blk", None, None),
            P("lvl", "blk", None, None),
            P("lvl", "blk", None, None, None),
            P("lvl", "blk", None, None, None),
            P(),
            P(),
            P(),
        ),
        out_specs=(P("lvl", "blk", None, None), P("lvl", "blk", None, None)),
        check_vma=False,
    )
```

```python
import jax
import jax.numpy as jnp
from jax import lax
from jax.sharding import PartitionSpec as P


def routing_tables(sources, owner, ranks):
    level_count, block_count = owner.shape
    position = jnp.arange(block_count, dtype=jnp.int32)
    tables = [None]
    for t in range(1, level_count):
        at_pos = (owner[t][None, :] == position[:, None]).astype(jnp.int32)
        src_block = jnp.sum(at_pos[:, :, None] * sources[t][None, :, :], axis=1)
        rank_pos = jnp.sum(at_pos[:, :, None] * ranks[t][None, :, :], axis=1)
        pick = (src_block[:, :, None] == position[None, None, :]).astype(jnp.int32)
        src_pos = jnp.sum(pick * owner[t - 1][None, None, :], axis=2)
        hit = (src_pos[:, None, :] == position[None, :, None]).astype(jnp.int32)
        target_of = jnp.sum(hit * position[:, None, None], axis=0)
        tables.append((src_pos, rank_pos, target_of))
    return tables


def mine(table, me):
    block_count = table.shape[0]
    row = (jnp.arange(block_count, dtype=jnp.int32) == me).astype(jnp.int32)
    return jnp.sum(row[:, None] * table, axis=0)


def one_hot(index, count, dtype):
    return (index[:, None] == jnp.arange(count, dtype=jnp.int32)[None, :]).astype(dtype)


def spread(out, src_row, row_count, my_row):
    width = out.shape[-1] // row_count
    piece = None
    for r in range(row_count):
        part = out[..., r * width:(r + 1) * width]
        if r == src_row:
            got = jnp.where(my_row == r, part, jnp.zeros_like(part))
        else:
            got = lax.ppermute(part, "lvl", [(src_row, r)])
        piece = got if piece is None else piece + got
    return piece


def collect(routed, dst_row, row_count):
    parts = []
    for r in range(row_count):
        if r == dst_row:
            parts.append(routed)
        else:
            parts.append(lax.ppermute(routed, "lvl", [(r, dst_row)]))
    return jnp.concatenate(parts, axis=-1)


def shift(array, by, row_count):
    return lax.ppermute(array, "lvl", [(i, (i + by) % row_count) for i in range(row_count)])


def one_hot_rows(index, count, dtype):
    return (jnp.arange(count, dtype=jnp.int32) == index).astype(dtype)


def blocks_of(level_blocks, my_row, by, row_count):
    wanted = lax.rem(my_row + by, row_count)
    chosen = level_blocks[0]
    for t in range(1, len(level_blocks)):
        chosen = jnp.where(wanted == t, level_blocks[t], chosen)
    return chosen


def of_level(parts, index):
    chosen = parts[0]
    for t in range(1, len(parts)):
        chosen = jnp.where(index == t, parts[t], chosen)
    return chosen


def take_block(full, index, count):
    width = full.shape[-1] // count
    blocks = full.reshape(full.shape[:-1] + (count, width))
    hot = (jnp.arange(count, dtype=jnp.int32) == index).astype(full.dtype)
    return jnp.sum(blocks * hot[:, None], axis=-2).astype(full.dtype)


def put_block(part, index, count):
    hot = (jnp.arange(count, dtype=jnp.int32) == index).astype(part.dtype)
    full = part[..., None, :] * hot[:, None]
    return full.reshape(part.shape[:-1] + (count * part.shape[-1],))


def pick_block(blocks, index, count):
    hot = (jnp.arange(count, dtype=jnp.int32) == index).astype(blocks.dtype)
    return jnp.sum(blocks * hot[None, :, None], axis=1).astype(blocks.dtype)


def frees_at(parts, my_row, t, row_count):
    pick = lax.rem(my_row - t + row_count, row_count)
    chosen = parts[0]
    for d in range(1, row_count):
        chosen = jnp.where(pick == d, parts[d], chosen)
    return chosen


def route(piece, send_to, take_from, block_count):
    send = one_hot(send_to, block_count, piece.dtype)
    holder = jnp.einsum("kj,krn->jrn", send, piece, preferred_element_type=jnp.float32)
    holder = holder.astype(piece.dtype)
    arrived = lax.all_to_all(holder, "blk", split_axis=0, concat_axis=0, tiled=True)
    take = one_hot(take_from, block_count, piece.dtype)
    routed = jnp.einsum("kj,jrn->krn", take, arrived, preferred_element_type=jnp.float32)
    return routed.astype(piece.dtype)


def local(rhs, inverse, left_factors, right_factors, sources, ranks, owner):
    assert rhs.shape[1] == 1
    level_count = sources.shape[0]
    block_count = owner.shape[1]
    row_count = lax.axis_size("lvl")
    rank_width = left_factors.shape[4]
    rhs_here = rhs[0, 0]
    inverse_here = inverse[0, 0]
    left_here = left_factors[0, 0]
    right_here = right_factors[0, 0]
    my_row = lax.axis_index("lvl")
    me = lax.axis_index("blk")
    tables = routing_tables(sources, owner, ranks)
    mine_src = [None] + [mine(tables[t][0], me) for t in range(1, level_count)]
    mine_rank = [None] + [mine(tables[t][1], me) for t in range(1, level_count)]
    mine_target = [None] + [mine(tables[t][2], me) for t in range(1, level_count)]
    lanes = jnp.arange(rank_width, dtype=jnp.int32)

    def keep_of(t):
        return (lanes[None, :] < mine_rank[t][:, None]).astype(jnp.float32)

    last = level_count - 1
    tile_count, block_rows, _ = left_here.shape
    columns = rhs_here.shape[-1]
    width = columns // row_count
    flat = tile_count * rank_width
    my_rank = jnp.zeros((tile_count,), jnp.int32)
    for t in range(1, level_count):
        my_rank = jnp.where(my_row == t, mine_rank[t], my_rank)
    keep = (lanes[None, :] < my_rank[:, None]).astype(left_here.dtype)
    left_flat = (left_here * keep[:, None, :]).transpose(1, 0, 2).reshape(block_rows, flat)
    right_flat = right_here.transpose(1, 0, 2).reshape(block_rows, flat)

    def dot(a, b, spec):
        return jnp.einsum(spec, a, b, preferred_element_type=jnp.float32)

    inv_left = dot(inverse_here, left_flat, "ab,bm->am").astype(jnp.bfloat16)
    couple = dot(right_flat, inv_left, "bq,bm->qm").astype(jnp.bfloat16)
    inv_rhs = dot(inverse_here, rhs_here, "ab,bn->an").astype(jnp.bfloat16)
    free = dot(right_flat, inv_rhs, "bq,bn->qn").astype(jnp.bfloat16)
    inv_left_f = inv_left
    gram = dot(inv_left_f, inv_left_f, "bq,bm->qm").astype(jnp.bfloat16)
    turn = dot(inv_left_f, inv_rhs, "bq,bn->qn").astype(jnp.bfloat16)
    couple = jnp.where(my_row == last, gram, couple)
    free = jnp.where(my_row == last, turn, free)
    couples = [couple] + [shift(couple, d, row_count) for d in range(1, row_count)]
    free_blocks = free.reshape(flat, row_count, width)
    frees = [pick_block(free_blocks, my_row, row_count)]
    for d in range(1, row_count):
        frees.append(shift(pick_block(free_blocks, lax.rem(my_row + d, row_count), row_count), d, row_count))

    def from_row(parts, t):
        pick = lax.rem(my_row - t + row_count, row_count)
        chosen = parts[row_count - 1]
        for d in reversed(range(row_count - 1)):
            chosen = jnp.where(pick == d, parts[d], chosen)
        return chosen

    def solve_forward(coef_full):
        lower = rhs_here.astype(jnp.float32) - dot(
            left_flat, coef_full.reshape(flat, columns), "bm,mn->bn"
        )
        return dot(inverse_here, lower.astype(jnp.bfloat16), "ab,bn->an").astype(jnp.bfloat16)

    def solve_backward(fwd, back_full):
        upper = fwd.astype(jnp.float32) - dot(
            right_flat, back_full.reshape(flat, columns), "bm,mn->bn"
        )
        return dot(inverse_here, upper.astype(jnp.bfloat16), "ba,bn->an").astype(jnp.bfloat16)

    lane_shape = (tile_count, rank_width, width)
    zero_block = jnp.zeros(lane_shape, jnp.bfloat16)

    def own_level_blocks(parts):
        full = put_block(of_level(parts, my_row), my_row, row_count)
        for d in range(1, row_count):
            got = shift(of_level(parts, lax.rem(my_row + d, row_count)), d, row_count)
            full = full + put_block(got, lax.rem(my_row - d + row_count, row_count), row_count)
        return full

    first = inv_rhs
    chain = [zero_block] * level_count
    start_block = frees_at(frees, my_row, 0, row_count).reshape(lane_shape)
    chain[1] = route(start_block, mine_target[1], mine_src[1], block_count)
    couple_at = [None] + [from_row(couples, t) for t in range(1, level_count)]
    for t in range(1, last):
        step = frees_at(frees, my_row, t, row_count).astype(jnp.float32) - dot(
            couple_at[t], chain[t].reshape(flat, width), "qm,mn->qn"
        )
        chain[t + 1] = route(step.astype(jnp.bfloat16).reshape(lane_shape), mine_target[t + 1], mine_src[t + 1], block_count)

    mine_fwd = solve_forward(own_level_blocks(chain))
    solved = jnp.where(my_row == 0, first, mine_fwd)
    top = dot(inverse_here, solved, "ba,bn->an").astype(jnp.bfloat16)
    back_term = dot(left_flat, top, "bm,bn->mn").astype(jnp.bfloat16)
    back_parts = [take_block(back_term, my_row, row_count)]
    for d in range(1, row_count):
        back_parts.append(shift(take_block(back_term, lax.rem(my_row + d, row_count), row_count), d, row_count))

    def back_free(t):
        return frees_at(back_parts, my_row, t, row_count)

    back = [zero_block] * level_count
    turned = frees_at(frees, my_row, last, row_count).astype(jnp.float32) - dot(
        couple_at[last], chain[last].reshape(flat, width), "qm,mn->qn"
    )
    back[last - 1] = route(turned.astype(jnp.bfloat16).reshape(lane_shape), mine_src[last], mine_target[last], block_count)
    for t in reversed(range(1, last)):
        step = back_free(t).astype(jnp.float32) - dot(
            couple_at[t], back[t - 0].reshape(flat, width), "mq,mn->qn"
        )
        back[t - 1] = route(step.astype(jnp.bfloat16).reshape(lane_shape), mine_src[t], mine_target[t], block_count)

    mine_back = solve_backward(solved, own_level_blocks(back[:last] + [zero_block]))
    answer = jnp.where(my_row == last, top, mine_back)
    return (solved[None, None], answer[None, None])


def solution(mesh):
    return jax.shard_map(
        local,
        mesh=mesh,
        in_specs=(
            P("lvl", "blk", None, None),
            P("lvl", "blk", None, None),
            P("lvl", "blk", None, None, None),
            P("lvl", "blk", None, None, None),
            P(),
            P(),
            P(),
        ),
        out_specs=(P("lvl", "blk", None, None), P("lvl", "blk", None, None)),
        check_vma=False,
    )
```

```python
import jax
import jax.numpy as jnp
from jax import lax
from jax.sharding import PartitionSpec as P


def routing_tables(sources, owner, ranks):
    level_count, block_count = owner.shape
    position = jnp.arange(block_count, dtype=jnp.int32)
    tables = [None]
    for t in range(1, level_count):
        at_pos = (owner[t][None, :] == position[:, None]).astype(jnp.int32)
        src_block = jnp.sum(at_pos[:, :, None] * sources[t][None, :, :], axis=1)
        rank_pos = jnp.sum(at_pos[:, :, None] * ranks[t][None, :, :], axis=1)
        pick = (src_block[:, :, None] == position[None, None, :]).astype(jnp.int32)
        src_pos = jnp.sum(pick * owner[t - 1][None, None, :], axis=2)
        hit = (src_pos[:, None, :] == position[None, :, None]).astype(jnp.int32)
        target_of = jnp.sum(hit * position[:, None, None], axis=0)
        tables.append((src_pos, rank_pos, target_of))
    return tables


def mine(table, me):
    block_count = table.shape[0]
    row = (jnp.arange(block_count, dtype=jnp.int32) == me).astype(jnp.int32)
    return jnp.sum(row[:, None] * table, axis=0)


def one_hot(index, count, dtype):
    return (index[:, None] == jnp.arange(count, dtype=jnp.int32)[None, :]).astype(dtype)


def spread(out, src_row, row_count, my_row):
    width = out.shape[-1] // row_count
    piece = None
    for r in range(row_count):
        part = out[..., r * width:(r + 1) * width]
        if r == src_row:
            got = jnp.where(my_row == r, part, jnp.zeros_like(part))
        else:
            got = lax.ppermute(part, "lvl", [(src_row, r)])
        piece = got if piece is None else piece + got
    return piece


def collect(routed, dst_row, row_count):
    parts = []
    for r in range(row_count):
        if r == dst_row:
            parts.append(routed)
        else:
            parts.append(lax.ppermute(routed, "lvl", [(r, dst_row)]))
    return jnp.concatenate(parts, axis=-1)


def shift(array, by, row_count):
    return lax.ppermute(array, "lvl", [(i, (i + by) % row_count) for i in range(row_count)])


def one_hot_rows(index, count, dtype):
    return (jnp.arange(count, dtype=jnp.int32) == index).astype(dtype)


def blocks_of(level_blocks, my_row, by, row_count):
    wanted = lax.rem(my_row + by, row_count)
    chosen = level_blocks[0]
    for t in range(1, len(level_blocks)):
        chosen = jnp.where(wanted == t, level_blocks[t], chosen)
    return chosen


def of_level(parts, index):
    chosen = parts[0]
    for t in range(1, len(parts)):
        chosen = jnp.where(index == t, parts[t], chosen)
    return chosen


def take_block(full, index, count):
    width = full.shape[-1] // count
    blocks = full.reshape(full.shape[:-1] + (count, width))
    hot = (jnp.arange(count, dtype=jnp.int32) == index).astype(full.dtype)
    return jnp.sum(blocks * hot[:, None], axis=-2).astype(full.dtype)


def put_block(part, index, count):
    hot = (jnp.arange(count, dtype=jnp.int32) == index).astype(part.dtype)
    full = part[..., None, :] * hot[:, None]
    return full.reshape(part.shape[:-1] + (count * part.shape[-1],))


def pick_block(blocks, index, count):
    hot = (jnp.arange(count, dtype=jnp.int32) == index).astype(blocks.dtype)
    return jnp.sum(blocks * hot[None, :, None], axis=1).astype(blocks.dtype)


def frees_at(parts, my_row, t, row_count):
    pick = lax.rem(my_row - t + row_count, row_count)
    chosen = parts[0]
    for d in range(1, row_count):
        chosen = jnp.where(pick == d, parts[d], chosen)
    return chosen


def route(piece, send_to, take_from, block_count):
    send = one_hot(send_to, block_count, piece.dtype)
    holder = jnp.einsum("kj,krn->jrn", send, piece, preferred_element_type=jnp.float32)
    holder = holder.astype(piece.dtype)
    arrived = lax.all_to_all(holder, "blk", split_axis=0, concat_axis=0, tiled=True)
    take = one_hot(take_from, block_count, piece.dtype)
    routed = jnp.einsum("kj,jrn->krn", take, arrived, preferred_element_type=jnp.float32)
    return routed.astype(piece.dtype)


def local(rhs, inverse, left_factors, right_factors, sources, ranks, owner):
    assert rhs.shape[1] == 1
    level_count = sources.shape[0]
    block_count = owner.shape[1]
    row_count = lax.axis_size("lvl")
    rank_width = left_factors.shape[4]
    rhs_here = rhs[0, 0]
    inverse_here = inverse[0, 0]
    left_here = left_factors[0, 0]
    right_here = right_factors[0, 0]
    my_row = lax.axis_index("lvl")
    me = lax.axis_index("blk")
    tables = routing_tables(sources, owner, ranks)
    mine_src = [None] + [mine(tables[t][0], me) for t in range(1, level_count)]
    mine_rank = [None] + [mine(tables[t][1], me) for t in range(1, level_count)]
    mine_target = [None] + [mine(tables[t][2], me) for t in range(1, level_count)]
    lanes = jnp.arange(rank_width, dtype=jnp.int32)

    def keep_of(t):
        return (lanes[None, :] < mine_rank[t][:, None]).astype(jnp.float32)

    last = level_count - 1
    tile_count, block_rows, _ = left_here.shape
    columns = rhs_here.shape[-1]
    width = columns // row_count
    flat = tile_count * rank_width
    my_rank = jnp.zeros((tile_count,), jnp.int32)
    for t in range(1, level_count):
        my_rank = jnp.where(my_row == t, mine_rank[t], my_rank)
    keep = (lanes[None, :] < my_rank[:, None]).astype(left_here.dtype)
    left_flat = (left_here * keep[:, None, :]).transpose(1, 0, 2).reshape(block_rows, flat)
    right_flat = right_here.transpose(1, 0, 2).reshape(block_rows, flat)

    def dot(a, b, spec):
        return jnp.einsum(spec, a, b, preferred_element_type=jnp.float32)

    inv_left = dot(inverse_here, left_flat, "ab,bm->am").astype(jnp.bfloat16)
    couple = dot(right_flat, inv_left, "bq,bm->qm").astype(jnp.bfloat16)
    inv_rhs = dot(inverse_here, rhs_here, "ab,bn->an").astype(jnp.bfloat16)
    free = dot(right_flat, inv_rhs, "bq,bn->qn").astype(jnp.bfloat16)
    gram = dot(inv_left, inv_left, "bq,bm->qm").astype(jnp.bfloat16)
    turn = dot(inv_left, inv_rhs, "bq,bn->qn").astype(jnp.bfloat16)
    couples = [couple] + [shift(couple, d, row_count) for d in range(1, row_count)]
    grams = [gram] + [shift(gram, d, row_count) for d in range(1, row_count)]

    def both_blocks(index):
        return jnp.concatenate(
            [take_block(free, index, row_count), take_block(turn, index, row_count)], axis=1
        )

    frees = [both_blocks(my_row)]
    for d in range(1, row_count):
        frees.append(shift(both_blocks(lax.rem(my_row + d, row_count)), d, row_count))

    def from_row(parts, t):
        pick = lax.rem(my_row - t + row_count, row_count)
        chosen = parts[row_count - 1]
        for d in reversed(range(row_count - 1)):
            chosen = jnp.where(pick == d, parts[d], chosen)
        return chosen

    def solve_forward(coef_full):
        lower = rhs_here.astype(jnp.float32) - dot(
            left_flat, coef_full.reshape(flat, columns), "bm,mn->bn"
        )
        return dot(inverse_here, lower.astype(jnp.bfloat16), "ab,bn->an").astype(jnp.bfloat16)

    def solve_backward(fwd, back_full):
        upper = fwd.astype(jnp.float32) - dot(
            right_flat, back_full.reshape(flat, columns), "bm,mn->bn"
        )
        return dot(inverse_here, upper.astype(jnp.bfloat16), "ba,bn->an").astype(jnp.bfloat16)

    lane_shape = (tile_count, rank_width, width)
    zero_block = jnp.zeros(lane_shape, jnp.bfloat16)

    def own_level_blocks(parts):
        full = put_block(of_level(parts, my_row), my_row, row_count)
        for d in range(1, row_count):
            got = shift(of_level(parts, lax.rem(my_row + d, row_count)), d, row_count)
            full = full + put_block(got, lax.rem(my_row - d + row_count, row_count), row_count)
        return full

    first = inv_rhs
    chain = [zero_block] * level_count
    start_block = frees_at(frees, my_row, 0, row_count)[:, :width].reshape(lane_shape)
    chain[1] = route(start_block, mine_target[1], mine_src[1], block_count)
    couple_at = [None] + [from_row(couples, t) for t in range(1, level_count)]
    for t in range(1, last):
        step = frees_at(frees, my_row, t, row_count)[:, :width].astype(jnp.float32) - dot(
            couple_at[t], chain[t].reshape(flat, width), "qm,mn->qn"
        )
        chain[t + 1] = route(step.astype(jnp.bfloat16).reshape(lane_shape), mine_target[t + 1], mine_src[t + 1], block_count)

    mine_fwd = solve_forward(own_level_blocks(chain))
    solved = jnp.where(my_row == 0, first, mine_fwd)
    top = dot(inverse_here, solved, "ba,bn->an").astype(jnp.bfloat16)
    gram_at = [None] + [from_row(grams, t) for t in range(1, level_count)]

    def back_free(t):
        return frees_at(frees, my_row, t, row_count)[:, width:].astype(jnp.float32) - dot(
            gram_at[t], chain[t].reshape(flat, width), "qm,mn->qn"
        )

    back_terms = [None] + [back_free(t) for t in range(1, level_count)]

    back = [zero_block] * level_count
    back[last - 1] = route(back_terms[last].astype(jnp.bfloat16).reshape(lane_shape), mine_src[last], mine_target[last], block_count)
    for t in reversed(range(1, last)):
        step = back_terms[t] - dot(
            couple_at[t], back[t - 0].reshape(flat, width), "mq,mn->qn"
        )
        back[t - 1] = route(step.astype(jnp.bfloat16).reshape(lane_shape), mine_src[t], mine_target[t], block_count)

    mine_back = solve_backward(solved, own_level_blocks(back[:last] + [zero_block]))
    answer = jnp.where(my_row == last, top, mine_back)
    return (solved[None, None], answer[None, None])


def solution(mesh):
    return jax.shard_map(
        local,
        mesh=mesh,
        in_specs=(
            P("lvl", "blk", None, None),
            P("lvl", "blk", None, None),
            P("lvl", "blk", None, None, None),
            P("lvl", "blk", None, None, None),
            P(),
            P(),
            P(),
        ),
        out_specs=(P("lvl", "blk", None, None), P("lvl", "blk", None, None)),
        check_vma=False,
    )
```

```python
import jax
import jax.numpy as jnp
from jax import lax
from jax.sharding import PartitionSpec as P


def routing_tables(sources, owner, ranks):
    level_count, block_count = owner.shape
    position = jnp.arange(block_count, dtype=jnp.int32)
    tables = [None]
    for t in range(1, level_count):
        at_pos = (owner[t][None, :] == position[:, None]).astype(jnp.int32)
        src_block = jnp.sum(at_pos[:, :, None] * sources[t][None, :, :], axis=1)
        rank_pos = jnp.sum(at_pos[:, :, None] * ranks[t][None, :, :], axis=1)
        pick = (src_block[:, :, None] == position[None, None, :]).astype(jnp.int32)
        src_pos = jnp.sum(pick * owner[t - 1][None, None, :], axis=2)
        hit = (src_pos[:, None, :] == position[None, :, None]).astype(jnp.int32)
        target_of = jnp.sum(hit * position[:, None, None], axis=0)
        tables.append((src_pos, rank_pos, target_of))
    return tables


def mine(table, me):
    block_count = table.shape[0]
    row = (jnp.arange(block_count, dtype=jnp.int32) == me).astype(jnp.int32)
    return jnp.sum(row[:, None] * table, axis=0)


def one_hot(index, count, dtype):
    return (index[:, None] == jnp.arange(count, dtype=jnp.int32)[None, :]).astype(dtype)


def spread(out, src_row, row_count, my_row):
    width = out.shape[-1] // row_count
    piece = None
    for r in range(row_count):
        part = out[..., r * width:(r + 1) * width]
        if r == src_row:
            got = jnp.where(my_row == r, part, jnp.zeros_like(part))
        else:
            got = lax.ppermute(part, "lvl", [(src_row, r)])
        piece = got if piece is None else piece + got
    return piece


def collect(routed, dst_row, row_count):
    parts = []
    for r in range(row_count):
        if r == dst_row:
            parts.append(routed)
        else:
            parts.append(lax.ppermute(routed, "lvl", [(r, dst_row)]))
    return jnp.concatenate(parts, axis=-1)


def shift(array, by, row_count):
    return lax.ppermute(array, "lvl", [(i, (i + by) % row_count) for i in range(row_count)])


def one_hot_rows(index, count, dtype):
    return (jnp.arange(count, dtype=jnp.int32) == index).astype(dtype)


def blocks_of(level_blocks, my_row, by, row_count):
    wanted = lax.rem(my_row + by, row_count)
    chosen = level_blocks[0]
    for t in range(1, len(level_blocks)):
        chosen = jnp.where(wanted == t, level_blocks[t], chosen)
    return chosen


def of_level(parts, index):
    chosen = parts[0]
    for t in range(1, len(parts)):
        chosen = jnp.where(index == t, parts[t], chosen)
    return chosen


def take_block(full, index, count):
    width = full.shape[-1] // count
    blocks = full.reshape(full.shape[:-1] + (count, width))
    hot = (jnp.arange(count, dtype=jnp.int32) == index).astype(full.dtype)
    return jnp.sum(blocks * hot[:, None], axis=-2).astype(full.dtype)


def put_block(part, index, count):
    hot = (jnp.arange(count, dtype=jnp.int32) == index).astype(part.dtype)
    full = part[..., None, :] * hot[:, None]
    return full.reshape(part.shape[:-1] + (count * part.shape[-1],))


def pick_block(blocks, index, count):
    hot = (jnp.arange(count, dtype=jnp.int32) == index).astype(blocks.dtype)
    return jnp.sum(blocks * hot[None, :, None], axis=1).astype(blocks.dtype)


def frees_at(parts, my_row, t, row_count):
    pick = lax.rem(my_row - t + row_count, row_count)
    chosen = parts[0]
    for d in range(1, row_count):
        chosen = jnp.where(pick == d, parts[d], chosen)
    return chosen


def route(piece, send_to, take_from, block_count):
    send = one_hot(send_to, block_count, piece.dtype)
    holder = jnp.einsum("kj,krn->jrn", send, piece, preferred_element_type=jnp.float32)
    holder = holder.astype(piece.dtype)
    arrived = lax.all_to_all(holder, "blk", split_axis=0, concat_axis=0, tiled=True)
    take = one_hot(take_from, block_count, piece.dtype)
    routed = jnp.einsum("kj,jrn->krn", take, arrived, preferred_element_type=jnp.float32)
    return routed.astype(piece.dtype)


def local(rhs, inverse, left_factors, right_factors, sources, ranks, owner):
    assert rhs.shape[1] == 1
    level_count = sources.shape[0]
    block_count = owner.shape[1]
    row_count = lax.axis_size("lvl")
    rank_width = left_factors.shape[4]
    rhs_here = rhs[0, 0]
    inverse_here = inverse[0, 0]
    left_here = left_factors[0, 0]
    right_here = right_factors[0, 0]
    my_row = lax.axis_index("lvl")
    me = lax.axis_index("blk")
    tables = routing_tables(sources, owner, ranks)
    mine_src = [None] + [mine(tables[t][0], me) for t in range(1, level_count)]
    mine_rank = [None] + [mine(tables[t][1], me) for t in range(1, level_count)]
    mine_target = [None] + [mine(tables[t][2], me) for t in range(1, level_count)]
    lanes = jnp.arange(rank_width, dtype=jnp.int32)

    def keep_of(t):
        return (lanes[None, :] < mine_rank[t][:, None]).astype(jnp.float32)

    last = level_count - 1
    tile_count, block_rows, _ = left_here.shape
    columns = rhs_here.shape[-1]
    width = columns // row_count
    flat = tile_count * rank_width
    my_rank = jnp.zeros((tile_count,), jnp.int32)
    for t in range(1, level_count):
        my_rank = jnp.where(my_row == t, mine_rank[t], my_rank)
    keep = (lanes[None, :] < my_rank[:, None]).astype(left_here.dtype)
    left_flat = (left_here * keep[:, None, :]).transpose(1, 0, 2).reshape(block_rows, flat)
    right_flat = right_here.transpose(1, 0, 2).reshape(block_rows, flat)

    def dot(a, b, spec):
        return jnp.einsum(spec, a, b, preferred_element_type=jnp.float32)

    inv_left = dot(inverse_here, left_flat, "ab,bm->am").astype(jnp.bfloat16)
    couple = dot(right_flat, inv_left, "bq,bm->qm").astype(jnp.bfloat16)
    inv_rhs = dot(inverse_here, rhs_here, "ab,bn->an").astype(jnp.bfloat16)
    free = dot(right_flat, inv_rhs, "bq,bn->qn").astype(jnp.bfloat16)
    gram = dot(inv_left, inv_left, "bq,bm->qm").astype(jnp.bfloat16)
    turn = dot(inv_left, inv_rhs, "bq,bn->qn").astype(jnp.bfloat16)
    couples = [couple] + [shift(couple, d, row_count) for d in range(1, row_count)]
    free_blocks = free.reshape(flat, row_count, width)
    frees = [pick_block(free_blocks, my_row, row_count)]
    for d in range(1, row_count):
        frees.append(shift(pick_block(free_blocks, lax.rem(my_row + d, row_count), row_count), d, row_count))

    def from_row(parts, t):
        pick = lax.rem(my_row - t + row_count, row_count)
        chosen = parts[row_count - 1]
        for d in reversed(range(row_count - 1)):
            chosen = jnp.where(pick == d, parts[d], chosen)
        return chosen

    def solve_forward(coef_full):
        lower = rhs_here.astype(jnp.float32) - dot(
            left_flat, coef_full.reshape(flat, columns), "bm,mn->bn"
        )
        return dot(inverse_here, lower.astype(jnp.bfloat16), "ab,bn->an").astype(jnp.bfloat16)

    def solve_backward(fwd, back_full):
        upper = fwd.astype(jnp.float32) - dot(
            right_flat, back_full.reshape(flat, columns), "bm,mn->bn"
        )
        return dot(inverse_here, upper.astype(jnp.bfloat16), "ba,bn->an").astype(jnp.bfloat16)

    lane_shape = (tile_count, rank_width, width)
    zero_block = jnp.zeros(lane_shape, jnp.bfloat16)

    def own_level_blocks(parts):
        full = put_block(of_level(parts, my_row), my_row, row_count)
        for d in range(1, row_count):
            got = shift(of_level(parts, lax.rem(my_row + d, row_count)), d, row_count)
            full = full + put_block(got, lax.rem(my_row - d + row_count, row_count), row_count)
        return full

    first = inv_rhs
    chain = [zero_block] * level_count
    start_block = frees_at(frees, my_row, 0, row_count).reshape(lane_shape)
    chain[1] = route(start_block, mine_target[1], mine_src[1], block_count)
    couple_at = [None] + [from_row(couples, t) for t in range(1, level_count)]
    grams = []
    for d in range(row_count):
        part = jnp.concatenate(
            [gram, take_block(turn, lax.rem(my_row + d, row_count), row_count)], axis=1
        )
        if d:
            part, _ = lax.optimization_barrier((part, chain[1]))
            part = shift(part, d, row_count)
        grams.append(part)
    gram_at = [None] + [from_row(grams, t) for t in range(1, level_count)]

    def back_free(t):
        return gram_at[t][:, flat:].astype(jnp.float32) - dot(
            gram_at[t][:, :flat], chain[t].reshape(flat, width), "qm,mn->qn"
        )

    for t in range(1, last):
        step = frees_at(frees, my_row, t, row_count).astype(jnp.float32) - dot(
            couple_at[t], chain[t].reshape(flat, width), "qm,mn->qn"
        )
        chain[t + 1] = route(step.astype(jnp.bfloat16).reshape(lane_shape), mine_target[t + 1], mine_src[t + 1], block_count)

    mine_fwd = solve_forward(own_level_blocks(chain))
    solved = jnp.where(my_row == 0, first, mine_fwd)
    top = dot(inverse_here, solved, "ba,bn->an").astype(jnp.bfloat16)

    back = [zero_block] * level_count
    back[last - 1] = route(back_free(last).astype(jnp.bfloat16).reshape(lane_shape), mine_src[last], mine_target[last], block_count)
    for t in reversed(range(1, last)):
        step = back_free(t) - dot(
            couple_at[t], back[t - 0].reshape(flat, width), "mq,mn->qn"
        )
        back[t - 1] = route(step.astype(jnp.bfloat16).reshape(lane_shape), mine_src[t], mine_target[t], block_count)

    mine_back = solve_backward(solved, own_level_blocks(back[:last] + [zero_block]))
    answer = jnp.where(my_row == last, top, mine_back)
    return (solved[None, None], answer[None, None])


def solution(mesh):
    return jax.shard_map(
        local,
        mesh=mesh,
        in_specs=(
            P("lvl", "blk", None, None),
            P("lvl", "blk", None, None),
            P("lvl", "blk", None, None, None),
            P("lvl", "blk", None, None, None),
            P(),
            P(),
            P(),
        ),
        out_specs=(P("lvl", "blk", None, None), P("lvl", "blk", None, None)),
        check_vma=False,
    )
```

```python
import jax
import jax.numpy as jnp
from jax import lax
from jax.sharding import PartitionSpec as P


def routing_tables(sources, owner, ranks):
    level_count, block_count = owner.shape
    position = jnp.arange(block_count, dtype=jnp.int32)
    tables = [None]
    for t in range(1, level_count):
        at_pos = (owner[t][None, :] == position[:, None]).astype(jnp.int32)
        src_block = jnp.sum(at_pos[:, :, None] * sources[t][None, :, :], axis=1)
        rank_pos = jnp.sum(at_pos[:, :, None] * ranks[t][None, :, :], axis=1)
        pick = (src_block[:, :, None] == position[None, None, :]).astype(jnp.int32)
        src_pos = jnp.sum(pick * owner[t - 1][None, None, :], axis=2)
        hit = (src_pos[:, None, :] == position[None, :, None]).astype(jnp.int32)
        target_of = jnp.sum(hit * position[:, None, None], axis=0)
        tables.append((src_pos, rank_pos, target_of))
    return tables


def mine(table, me):
    block_count = table.shape[0]
    row = (jnp.arange(block_count, dtype=jnp.int32) == me).astype(jnp.int32)
    return jnp.sum(row[:, None] * table, axis=0)


def one_hot(index, count, dtype):
    return (index[:, None] == jnp.arange(count, dtype=jnp.int32)[None, :]).astype(dtype)


def spread(out, src_row, row_count, my_row):
    width = out.shape[-1] // row_count
    piece = None
    for r in range(row_count):
        part = out[..., r * width:(r + 1) * width]
        if r == src_row:
            got = jnp.where(my_row == r, part, jnp.zeros_like(part))
        else:
            got = lax.ppermute(part, "lvl", [(src_row, r)])
        piece = got if piece is None else piece + got
    return piece


def collect(routed, dst_row, row_count):
    parts = []
    for r in range(row_count):
        if r == dst_row:
            parts.append(routed)
        else:
            parts.append(lax.ppermute(routed, "lvl", [(r, dst_row)]))
    return jnp.concatenate(parts, axis=-1)


def shift(array, by, row_count):
    return lax.ppermute(array, "lvl", [(i, (i + by) % row_count) for i in range(row_count)])


def one_hot_rows(index, count, dtype):
    return (jnp.arange(count, dtype=jnp.int32) == index).astype(dtype)


def blocks_of(level_blocks, my_row, by, row_count):
    wanted = lax.rem(my_row + by, row_count)
    chosen = level_blocks[0]
    for t in range(1, len(level_blocks)):
        chosen = jnp.where(wanted == t, level_blocks[t], chosen)
    return chosen


def of_level(parts, index):
    chosen = parts[0]
    for t in range(1, len(parts)):
        chosen = jnp.where(index == t, parts[t], chosen)
    return chosen


def take_block(full, index, count):
    width = full.shape[-1] // count
    blocks = full.reshape(full.shape[:-1] + (count, width))
    hot = (jnp.arange(count, dtype=jnp.int32) == index).astype(full.dtype)
    return jnp.sum(blocks * hot[:, None], axis=-2).astype(full.dtype)


def put_block(part, index, count):
    hot = (jnp.arange(count, dtype=jnp.int32) == index).astype(part.dtype)
    full = part[..., None, :] * hot[:, None]
    return full.reshape(part.shape[:-1] + (count * part.shape[-1],))


def pick_block(blocks, index, count):
    hot = (jnp.arange(count, dtype=jnp.int32) == index).astype(blocks.dtype)
    return jnp.sum(blocks * hot[None, :, None], axis=1).astype(blocks.dtype)


def frees_at(parts, my_row, t, row_count):
    pick = lax.rem(my_row - t + row_count, row_count)
    chosen = parts[0]
    for d in range(1, row_count):
        chosen = jnp.where(pick == d, parts[d], chosen)
    return chosen


def route(piece, send_to, take_from, block_count):
    send = one_hot(send_to, block_count, piece.dtype)
    holder = jnp.einsum("kj,krn->jrn", send, piece, preferred_element_type=jnp.float32)
    holder = holder.astype(piece.dtype)
    arrived = lax.all_to_all(holder, "blk", split_axis=0, concat_axis=0, tiled=True)
    take = one_hot(take_from, block_count, piece.dtype)
    routed = jnp.einsum("kj,jrn->krn", take, arrived, preferred_element_type=jnp.float32)
    return routed.astype(piece.dtype)


def local(rhs, inverse, left_factors, right_factors, sources, ranks, owner):
    assert rhs.shape[1] == 1
    level_count = sources.shape[0]
    block_count = owner.shape[1]
    row_count = lax.axis_size("lvl")
    rank_width = left_factors.shape[4]
    rhs_here = rhs[0, 0]
    inverse_here = inverse[0, 0]
    left_here = left_factors[0, 0]
    right_here = right_factors[0, 0]
    my_row = lax.axis_index("lvl")
    me = lax.axis_index("blk")
    tables = routing_tables(sources, owner, ranks)
    mine_src = [None] + [mine(tables[t][0], me) for t in range(1, level_count)]
    mine_rank = [None] + [mine(tables[t][1], me) for t in range(1, level_count)]
    mine_target = [None] + [mine(tables[t][2], me) for t in range(1, level_count)]
    lanes = jnp.arange(rank_width, dtype=jnp.int32)

    def keep_of(t):
        return (lanes[None, :] < mine_rank[t][:, None]).astype(jnp.float32)

    last = level_count - 1
    tile_count, block_rows, _ = left_here.shape
    columns = rhs_here.shape[-1]
    width = columns // row_count
    flat = tile_count * rank_width
    my_rank = jnp.zeros((tile_count,), jnp.int32)
    for t in range(1, level_count):
        my_rank = jnp.where(my_row == t, mine_rank[t], my_rank)
    keep = (lanes[None, :] < my_rank[:, None]).astype(left_here.dtype)
    left_flat = (left_here * keep[:, None, :]).transpose(1, 0, 2).reshape(block_rows, flat)
    right_flat = right_here.transpose(1, 0, 2).reshape(block_rows, flat)

    def dot(a, b, spec):
        return jnp.einsum(spec, a, b, preferred_element_type=jnp.float32)

    inv_left = dot(inverse_here, left_flat, "ab,bm->am").astype(jnp.bfloat16)
    couple = dot(right_flat, inv_left, "bq,bm->qm").astype(jnp.bfloat16)
    inv_rhs = dot(inverse_here, rhs_here, "ab,bn->an").astype(jnp.bfloat16)
    free = dot(right_flat, inv_rhs, "bq,bn->qn").astype(jnp.bfloat16)
    gram = dot(inv_left, inv_left, "bq,bm->qm").astype(jnp.bfloat16)
    turn = dot(inv_left, inv_rhs, "bq,bn->qn").astype(jnp.bfloat16)
    couples = [couple] + [shift(couple, d, row_count) for d in range(1, row_count)]
    free_blocks = free.reshape(flat, row_count, width)
    frees = [pick_block(free_blocks, my_row, row_count)]
    for d in range(1, row_count):
        frees.append(shift(pick_block(free_blocks, lax.rem(my_row + d, row_count), row_count), d, row_count))

    def from_row(parts, t):
        pick = lax.rem(my_row - t + row_count, row_count)
        chosen = parts[row_count - 1]
        for d in reversed(range(row_count - 1)):
            chosen = jnp.where(pick == d, parts[d], chosen)
        return chosen

    def solve_forward(coef_full):
        lower = rhs_here.astype(jnp.float32) - dot(
            left_flat, coef_full.reshape(flat, columns), "bm,mn->bn"
        )
        return dot(inverse_here, lower.astype(jnp.bfloat16), "ab,bn->an").astype(jnp.bfloat16)

    def solve_backward(fwd, back_full):
        upper = fwd.astype(jnp.float32) - dot(
            right_flat, back_full.reshape(flat, columns), "bm,mn->bn"
        )
        return dot(inverse_here, upper.astype(jnp.bfloat16), "ba,bn->an").astype(jnp.bfloat16)

    lane_shape = (tile_count, rank_width, width)
    zero_block = jnp.zeros(lane_shape, jnp.bfloat16)

    def own_level_blocks(parts):
        full = put_block(of_level(parts, my_row), my_row, row_count)
        for d in range(1, row_count):
            got = shift(of_level(parts, lax.rem(my_row + d, row_count)), d, row_count)
            full = full + put_block(got, lax.rem(my_row - d + row_count, row_count), row_count)
        return full

    first = inv_rhs
    chain = [zero_block] * level_count
    start_block = frees_at(frees, my_row, 0, row_count).reshape(lane_shape)
    chain[1] = route(start_block, mine_target[1], mine_src[1], block_count)
    couple_at = [None] + [from_row(couples, t) for t in range(1, level_count)]
    grams = []
    for d in range(row_count):
        part = jnp.concatenate(
            [gram, take_block(turn, lax.rem(my_row + d, row_count), row_count)], axis=1
        )
        if d:
            part, _ = lax.optimization_barrier((part, couple_at[1]))
            part = shift(part, d, row_count)
        grams.append(part)
    gram_at = [None] + [from_row(grams, t) for t in range(1, level_count)]

    def back_free(t):
        return gram_at[t][:, flat:].astype(jnp.float32) - dot(
            gram_at[t][:, :flat], chain[t].reshape(flat, width), "qm,mn->qn"
        )

    for t in range(1, last):
        step = frees_at(frees, my_row, t, row_count).astype(jnp.float32) - dot(
            couple_at[t], chain[t].reshape(flat, width), "qm,mn->qn"
        )
        chain[t + 1] = route(step.astype(jnp.bfloat16).reshape(lane_shape), mine_target[t + 1], mine_src[t + 1], block_count)

    mine_fwd = solve_forward(own_level_blocks(chain))
    solved = jnp.where(my_row == 0, first, mine_fwd)
    top = dot(inverse_here, solved, "ba,bn->an").astype(jnp.bfloat16)

    back = [zero_block] * level_count
    back[last - 1] = route(back_free(last).astype(jnp.bfloat16).reshape(lane_shape), mine_src[last], mine_target[last], block_count)
    for t in reversed(range(1, last)):
        step = back_free(t) - dot(
            couple_at[t], back[t - 0].reshape(flat, width), "mq,mn->qn"
        )
        back[t - 1] = route(step.astype(jnp.bfloat16).reshape(lane_shape), mine_src[t], mine_target[t], block_count)

    mine_back = solve_backward(solved, own_level_blocks(back[:last] + [zero_block]))
    answer = jnp.where(my_row == last, top, mine_back)
    return (solved[None, None], answer[None, None])


def solution(mesh):
    return jax.shard_map(
        local,
        mesh=mesh,
        in_specs=(
            P("lvl", "blk", None, None),
            P("lvl", "blk", None, None),
            P("lvl", "blk", None, None, None),
            P("lvl", "blk", None, None, None),
            P(),
            P(),
            P(),
        ),
        out_specs=(P("lvl", "blk", None, None), P("lvl", "blk", None, None)),
        check_vma=False,
    )
```

```python
import jax
import jax.numpy as jnp
from jax import lax
from jax.sharding import PartitionSpec as P


def routing_tables(sources, owner, ranks):
    level_count, block_count = owner.shape
    position = jnp.arange(block_count, dtype=jnp.int32)
    tables = [None]
    for t in range(1, level_count):
        at_pos = (owner[t][None, :] == position[:, None]).astype(jnp.int32)
        src_block = jnp.sum(at_pos[:, :, None] * sources[t][None, :, :], axis=1)
        rank_pos = jnp.sum(at_pos[:, :, None] * ranks[t][None, :, :], axis=1)
        pick = (src_block[:, :, None] == position[None, None, :]).astype(jnp.int32)
        src_pos = jnp.sum(pick * owner[t - 1][None, None, :], axis=2)
        hit = (src_pos[:, None, :] == position[None, :, None]).astype(jnp.int32)
        target_of = jnp.sum(hit * position[:, None, None], axis=0)
        tables.append((src_pos, rank_pos, target_of))
    return tables


def mine(table, me):
    block_count = table.shape[0]
    row = (jnp.arange(block_count, dtype=jnp.int32) == me).astype(jnp.int32)
    return jnp.sum(row[:, None] * table, axis=0)


def one_hot(index, count, dtype):
    return (index[:, None] == jnp.arange(count, dtype=jnp.int32)[None, :]).astype(dtype)


def spread(out, src_row, row_count, my_row):
    width = out.shape[-1] // row_count
    piece = None
    for r in range(row_count):
        part = out[..., r * width:(r + 1) * width]
        if r == src_row:
            got = jnp.where(my_row == r, part, jnp.zeros_like(part))
        else:
            got = lax.ppermute(part, "lvl", [(src_row, r)])
        piece = got if piece is None else piece + got
    return piece


def collect(routed, dst_row, row_count):
    parts = []
    for r in range(row_count):
        if r == dst_row:
            parts.append(routed)
        else:
            parts.append(lax.ppermute(routed, "lvl", [(r, dst_row)]))
    return jnp.concatenate(parts, axis=-1)


def shift(array, by, row_count):
    return lax.ppermute(array, "lvl", [(i, (i + by) % row_count) for i in range(row_count)])


def one_hot_rows(index, count, dtype):
    return (jnp.arange(count, dtype=jnp.int32) == index).astype(dtype)


def blocks_of(level_blocks, my_row, by, row_count):
    wanted = lax.rem(my_row + by, row_count)
    chosen = level_blocks[0]
    for t in range(1, len(level_blocks)):
        chosen = jnp.where(wanted == t, level_blocks[t], chosen)
    return chosen


def of_level(parts, index):
    chosen = parts[0]
    for t in range(1, len(parts)):
        chosen = jnp.where(index == t, parts[t], chosen)
    return chosen


def take_block(full, index, count):
    width = full.shape[-1] // count
    blocks = full.reshape(full.shape[:-1] + (count, width))
    hot = (jnp.arange(count, dtype=jnp.int32) == index).astype(full.dtype)
    return jnp.sum(blocks * hot[:, None], axis=-2).astype(full.dtype)


def put_block(part, index, count):
    hot = (jnp.arange(count, dtype=jnp.int32) == index).astype(part.dtype)
    full = part[..., None, :] * hot[:, None]
    return full.reshape(part.shape[:-1] + (count * part.shape[-1],))


def pick_block(blocks, index, count):
    hot = (jnp.arange(count, dtype=jnp.int32) == index).astype(blocks.dtype)
    return jnp.sum(blocks * hot[None, :, None], axis=1).astype(blocks.dtype)


def frees_at(parts, my_row, t, row_count):
    pick = lax.rem(my_row - t + row_count, row_count)
    chosen = parts[0]
    for d in range(1, row_count):
        chosen = jnp.where(pick == d, parts[d], chosen)
    return chosen


def route(piece, send_to, take_from, block_count):
    send = one_hot(send_to, block_count, piece.dtype)
    holder = jnp.einsum("kj,krn->jrn", send, piece, preferred_element_type=jnp.float32)
    holder = holder.astype(piece.dtype)
    arrived = lax.all_to_all(holder, "blk", split_axis=0, concat_axis=0, tiled=True)
    take = one_hot(take_from, block_count, piece.dtype)
    routed = jnp.einsum("kj,jrn->krn", take, arrived, preferred_element_type=jnp.float32)
    return routed.astype(piece.dtype)


def local(rhs, inverse, left_factors, right_factors, sources, ranks, owner):
    assert rhs.shape[1] == 1
    level_count = sources.shape[0]
    block_count = owner.shape[1]
    row_count = lax.axis_size("lvl")
    rank_width = left_factors.shape[4]
    rhs_here = rhs[0, 0]
    inverse_here = inverse[0, 0]
    left_here = left_factors[0, 0]
    right_here = right_factors[0, 0]
    my_row = lax.axis_index("lvl")
    me = lax.axis_index("blk")
    tables = routing_tables(sources, owner, ranks)
    mine_src = [None] + [mine(tables[t][0], me) for t in range(1, level_count)]
    mine_rank = [None] + [mine(tables[t][1], me) for t in range(1, level_count)]
    mine_target = [None] + [mine(tables[t][2], me) for t in range(1, level_count)]
    lanes = jnp.arange(rank_width, dtype=jnp.int32)

    def keep_of(t):
        return (lanes[None, :] < mine_rank[t][:, None]).astype(jnp.float32)

    last = level_count - 1
    tile_count, block_rows, _ = left_here.shape
    columns = rhs_here.shape[-1]
    width = columns // row_count
    flat = tile_count * rank_width
    my_rank = jnp.zeros((tile_count,), jnp.int32)
    for t in range(1, level_count):
        my_rank = jnp.where(my_row == t, mine_rank[t], my_rank)
    keep = (lanes[None, :] < my_rank[:, None]).astype(left_here.dtype)
    left_flat = (left_here * keep[:, None, :]).transpose(1, 0, 2).reshape(block_rows, flat)
    right_flat = right_here.transpose(1, 0, 2).reshape(block_rows, flat)

    def dot(a, b, spec):
        return jnp.einsum(spec, a, b, preferred_element_type=jnp.float32)

    inv_left = dot(inverse_here, left_flat, "ab,bm->am").astype(jnp.bfloat16)
    couple = dot(right_flat, inv_left, "bq,bm->qm").astype(jnp.bfloat16)
    inv_rhs = dot(inverse_here, rhs_here, "ab,bn->an").astype(jnp.bfloat16)
    free = dot(right_flat, inv_rhs, "bq,bn->qn").astype(jnp.bfloat16)
    gram = dot(inv_left, inv_left, "bq,bm->qm").astype(jnp.bfloat16)
    turn = dot(inv_left, inv_rhs, "bq,bn->qn").astype(jnp.bfloat16)
    couple = jnp.where(my_row == last, gram, couple)
    free = jnp.where(my_row == last, turn, free)
    couples = [couple] + [shift(couple, d, row_count) for d in range(1, row_count)]
    free_blocks = free.reshape(flat, row_count, width)
    frees = [pick_block(free_blocks, my_row, row_count)]
    for d in range(1, row_count):
        frees.append(shift(pick_block(free_blocks, lax.rem(my_row + d, row_count), row_count), d, row_count))

    def from_row(parts, t):
        pick = lax.rem(my_row - t + row_count, row_count)
        chosen = parts[row_count - 1]
        for d in reversed(range(row_count - 1)):
            chosen = jnp.where(pick == d, parts[d], chosen)
        return chosen

    def solve_forward(coef_full):
        lower = rhs_here.astype(jnp.float32) - dot(
            left_flat, coef_full.reshape(flat, columns), "bm,mn->bn"
        )
        return dot(inverse_here, lower.astype(jnp.bfloat16), "ab,bn->an").astype(jnp.bfloat16)

    def solve_backward(fwd, back_full):
        upper = fwd.astype(jnp.float32) - dot(
            right_flat, back_full.reshape(flat, columns), "bm,mn->bn"
        )
        return dot(inverse_here, upper.astype(jnp.bfloat16), "ba,bn->an").astype(jnp.bfloat16)

    lane_shape = (tile_count, rank_width, width)
    zero_block = jnp.zeros(lane_shape, jnp.bfloat16)

    def own_level_blocks(parts):
        full = put_block(of_level(parts, my_row), my_row, row_count)
        for d in range(1, row_count):
            got = shift(of_level(parts, lax.rem(my_row + d, row_count)), d, row_count)
            full = full + put_block(got, lax.rem(my_row - d + row_count, row_count), row_count)
        return full

    first = inv_rhs
    chain = [zero_block] * level_count
    start_block = frees_at(frees, my_row, 0, row_count).reshape(lane_shape)
    chain[1] = route(start_block, mine_target[1], mine_src[1], block_count)
    couple_at = [None] + [from_row(couples, t) for t in range(1, level_count)]
    grams = []
    for d in range(row_count):
        part = jnp.concatenate(
            [gram, take_block(turn, lax.rem(my_row + d, row_count), row_count)], axis=1
        )
        if d:
            part, _ = lax.optimization_barrier((part, couple_at[1]))
            part = shift(part, d, row_count)
        grams.append(part)
    gram_at = [None] + [from_row(grams, t) for t in range(1, last)]

    def back_free(t):
        return gram_at[t][:, flat:].astype(jnp.float32) - dot(
            gram_at[t][:, :flat], chain[t].reshape(flat, width), "qm,mn->qn"
        )

    for t in range(1, last):
        step = frees_at(frees, my_row, t, row_count).astype(jnp.float32) - dot(
            couple_at[t], chain[t].reshape(flat, width), "qm,mn->qn"
        )
        chain[t + 1] = route(step.astype(jnp.bfloat16).reshape(lane_shape), mine_target[t + 1], mine_src[t + 1], block_count)

    mine_fwd = solve_forward(own_level_blocks(chain))
    solved = jnp.where(my_row == 0, first, mine_fwd)
    top = dot(inverse_here, solved, "ba,bn->an").astype(jnp.bfloat16)

    back = [zero_block] * level_count
    turned = frees_at(frees, my_row, last, row_count).astype(jnp.float32) - dot(
        couple_at[last], chain[last].reshape(flat, width), "qm,mn->qn"
    )
    back[last - 1] = route(turned.astype(jnp.bfloat16).reshape(lane_shape), mine_src[last], mine_target[last], block_count)
    for t in reversed(range(1, last)):
        step = back_free(t) - dot(
            couple_at[t], back[t - 0].reshape(flat, width), "mq,mn->qn"
        )
        back[t - 1] = route(step.astype(jnp.bfloat16).reshape(lane_shape), mine_src[t], mine_target[t], block_count)

    mine_back = solve_backward(solved, own_level_blocks(back[:last] + [zero_block]))
    answer = jnp.where(my_row == last, top, mine_back)
    return (solved[None, None], answer[None, None])


def solution(mesh):
    return jax.shard_map(
        local,
        mesh=mesh,
        in_specs=(
            P("lvl", "blk", None, None),
            P("lvl", "blk", None, None),
            P("lvl", "blk", None, None, None),
            P("lvl", "blk", None, None, None),
            P(),
            P(),
            P(),
        ),
        out_specs=(P("lvl", "blk", None, None), P("lvl", "blk", None, None)),
        check_vma=False,
    )
```

```python
import jax
import jax.numpy as jnp
from jax import lax
from jax.sharding import PartitionSpec as P


def routing_tables(sources, owner, ranks):
    level_count, block_count = owner.shape
    position = jnp.arange(block_count, dtype=jnp.int32)
    tables = [None]
    for t in range(1, level_count):
        at_pos = (owner[t][None, :] == position[:, None]).astype(jnp.int32)
        src_block = jnp.sum(at_pos[:, :, None] * sources[t][None, :, :], axis=1)
        rank_pos = jnp.sum(at_pos[:, :, None] * ranks[t][None, :, :], axis=1)
        pick = (src_block[:, :, None] == position[None, None, :]).astype(jnp.int32)
        src_pos = jnp.sum(pick * owner[t - 1][None, None, :], axis=2)
        hit = (src_pos[:, None, :] == position[None, :, None]).astype(jnp.int32)
        target_of = jnp.sum(hit * position[:, None, None], axis=0)
        tables.append((src_pos, rank_pos, target_of))
    return tables


def mine(table, me):
    block_count = table.shape[0]
    row = (jnp.arange(block_count, dtype=jnp.int32) == me).astype(jnp.int32)
    return jnp.sum(row[:, None] * table, axis=0)


def one_hot(index, count, dtype):
    return (index[:, None] == jnp.arange(count, dtype=jnp.int32)[None, :]).astype(dtype)


def spread(out, src_row, row_count, my_row):
    width = out.shape[-1] // row_count
    piece = None
    for r in range(row_count):
        part = out[..., r * width:(r + 1) * width]
        if r == src_row:
            got = jnp.where(my_row == r, part, jnp.zeros_like(part))
        else:
            got = lax.ppermute(part, "lvl", [(src_row, r)])
        piece = got if piece is None else piece + got
    return piece


def collect(routed, dst_row, row_count):
    parts = []
    for r in range(row_count):
        if r == dst_row:
            parts.append(routed)
        else:
            parts.append(lax.ppermute(routed, "lvl", [(r, dst_row)]))
    return jnp.concatenate(parts, axis=-1)


def shift(array, by, row_count):
    return lax.ppermute(array, "lvl", [(i, (i + by) % row_count) for i in range(row_count)])


def one_hot_rows(index, count, dtype):
    return (jnp.arange(count, dtype=jnp.int32) == index).astype(dtype)


def blocks_of(level_blocks, my_row, by, row_count):
    wanted = lax.rem(my_row + by, row_count)
    chosen = level_blocks[0]
    for t in range(1, len(level_blocks)):
        chosen = jnp.where(wanted == t, level_blocks[t], chosen)
    return chosen


def of_level(parts, index):
    chosen = parts[0]
    for t in range(1, len(parts)):
        chosen = jnp.where(index == t, parts[t], chosen)
    return chosen


def take_block(full, index, count):
    width = full.shape[-1] // count
    blocks = full.reshape(full.shape[:-1] + (count, width))
    hot = (jnp.arange(count, dtype=jnp.int32) == index).astype(full.dtype)
    return jnp.sum(blocks * hot[:, None], axis=-2).astype(full.dtype)


def put_block(part, index, count):
    hot = (jnp.arange(count, dtype=jnp.int32) == index).astype(part.dtype)
    full = part[..., None, :] * hot[:, None]
    return full.reshape(part.shape[:-1] + (count * part.shape[-1],))


def pick_block(blocks, index, count):
    hot = (jnp.arange(count, dtype=jnp.int32) == index).astype(blocks.dtype)
    return jnp.sum(blocks * hot[None, :, None], axis=1).astype(blocks.dtype)


def frees_at(parts, my_row, t, row_count):
    pick = lax.rem(my_row - t + row_count, row_count)
    chosen = parts[0]
    for d in range(1, row_count):
        chosen = jnp.where(pick == d, parts[d], chosen)
    return chosen


def route(piece, send_to, take_from, block_count):
    send = one_hot(send_to, block_count, piece.dtype)
    holder = jnp.einsum("kj,krn->jrn", send, piece, preferred_element_type=jnp.float32)
    holder = holder.astype(piece.dtype)
    arrived = lax.all_to_all(holder, "blk", split_axis=0, concat_axis=0, tiled=True)
    take = one_hot(take_from, block_count, piece.dtype)
    routed = jnp.einsum("kj,jrn->krn", take, arrived, preferred_element_type=jnp.float32)
    return routed.astype(piece.dtype)


def local(rhs, inverse, left_factors, right_factors, sources, ranks, owner):
    assert rhs.shape[1] == 1
    level_count = sources.shape[0]
    block_count = owner.shape[1]
    row_count = lax.axis_size("lvl")
    rank_width = left_factors.shape[4]
    rhs_here = rhs[0, 0]
    inverse_here = inverse[0, 0]
    left_here = left_factors[0, 0]
    right_here = right_factors[0, 0]
    my_row = lax.axis_index("lvl")
    me = lax.axis_index("blk")
    tables = routing_tables(sources, owner, ranks)
    mine_src = [None] + [mine(tables[t][0], me) for t in range(1, level_count)]
    mine_rank = [None] + [mine(tables[t][1], me) for t in range(1, level_count)]
    mine_target = [None] + [mine(tables[t][2], me) for t in range(1, level_count)]
    lanes = jnp.arange(rank_width, dtype=jnp.int32)

    def keep_of(t):
        return (lanes[None, :] < mine_rank[t][:, None]).astype(jnp.float32)

    last = level_count - 1
    tile_count, block_rows, _ = left_here.shape
    columns = rhs_here.shape[-1]
    width = columns // row_count
    flat = tile_count * rank_width
    my_rank = jnp.zeros((tile_count,), jnp.int32)
    for t in range(1, level_count):
        my_rank = jnp.where(my_row == t, mine_rank[t], my_rank)
    keep = (lanes[None, :] < my_rank[:, None]).astype(left_here.dtype)
    left_flat = (left_here * keep[:, None, :]).transpose(1, 0, 2).reshape(block_rows, flat)
    right_flat = right_here.transpose(1, 0, 2).reshape(block_rows, flat)

    def dot(a, b, spec):
        return jnp.einsum(spec, a, b, preferred_element_type=jnp.float32)

    inv_left = dot(inverse_here, left_flat, "ab,bm->am").astype(jnp.bfloat16)
    couple = dot(right_flat, inv_left, "bq,bm->qm").astype(jnp.bfloat16)
    inv_rhs = dot(inverse_here, rhs_here, "ab,bn->an").astype(jnp.bfloat16)
    free = dot(right_flat, inv_rhs, "bq,bn->qn").astype(jnp.bfloat16)
    inv_left_f = inv_left
    gram = dot(inv_left_f, inv_left_f, "bq,bm->qm").astype(jnp.bfloat16)
    turn = dot(inv_left_f, inv_rhs, "bq,bn->qn").astype(jnp.bfloat16)
    couple = jnp.where(my_row == last, gram, couple)
    free = jnp.where(my_row == last, turn, free)
    couples = [couple] + [shift(couple, d, row_count) for d in range(1, row_count)]
    free_blocks = free.reshape(flat, row_count, width)
    frees = [pick_block(free_blocks, my_row, row_count)]
    for d in range(1, row_count):
        frees.append(shift(pick_block(free_blocks, lax.rem(my_row + d, row_count), row_count), d, row_count))

    def from_row(parts, t):
        pick = lax.rem(my_row - t + row_count, row_count)
        chosen = parts[row_count - 1]
        for d in reversed(range(row_count - 1)):
            chosen = jnp.where(pick == d, parts[d], chosen)
        return chosen

    def solve_forward(coef_full):
        lower = rhs_here.astype(jnp.float32) - dot(
            left_flat, coef_full.reshape(flat, columns), "bm,mn->bn"
        )
        return dot(inverse_here, lower.astype(jnp.bfloat16), "ab,bn->an").astype(jnp.bfloat16)

    def solve_backward(fwd, back_full):
        upper = fwd.astype(jnp.float32) - dot(
            right_flat, back_full.reshape(flat, columns), "bm,mn->bn"
        )
        return dot(inverse_here, upper.astype(jnp.bfloat16), "ba,bn->an").astype(jnp.bfloat16)

    lane_shape = (tile_count, rank_width, width)
    zero_block = jnp.zeros(lane_shape, jnp.bfloat16)

    def own_level_blocks(parts):
        full = put_block(of_level(parts, my_row), my_row, row_count)
        for d in range(1, row_count):
            got = shift(of_level(parts, lax.rem(my_row + d, row_count)), d, row_count)
            full = full + put_block(got, lax.rem(my_row - d + row_count, row_count), row_count)
        return full

    first = inv_rhs
    chain = [zero_block] * level_count
    start_block = frees_at(frees, my_row, 0, row_count).reshape(lane_shape)
    chain[1] = route(start_block, mine_target[1], mine_src[1], block_count)
    couple_at = [None] + [from_row(couples, t) for t in range(1, level_count)]
    for t in range(1, last):
        step = frees_at(frees, my_row, t, row_count).astype(jnp.float32) - dot(
            couple_at[t], chain[t].reshape(flat, width), "qm,mn->qn"
        )
        chain[t + 1] = route(step.astype(jnp.bfloat16).reshape(lane_shape), mine_target[t + 1], mine_src[t + 1], block_count)

    lower_chain = [zero_block] + chain[1:last] + [zero_block]
    early_fwd = solve_forward(own_level_blocks(lower_chain))
    inv_t_early = dot(inverse_here, early_fwd, "ba,bn->an").astype(jnp.bfloat16)
    back_term = dot(left_flat, inv_t_early, "bm,bn->mn").astype(jnp.bfloat16)
    top_fwd = solve_forward(collect(chain[last], last, row_count))
    mine_fwd = jnp.where(my_row == last, top_fwd, early_fwd)
    solved = jnp.where(my_row == 0, first, mine_fwd)
    top = dot(inverse_here, solved, "ba,bn->an").astype(jnp.bfloat16)
    back_parts = [take_block(back_term, my_row, row_count)]
    for d in range(1, row_count):
        back_parts.append(shift(take_block(back_term, lax.rem(my_row + d, row_count), row_count), d, row_count))

    def back_free(t):
        return frees_at(back_parts, my_row, t, row_count)

    back = [zero_block] * level_count
    turned = frees_at(frees, my_row, last, row_count).astype(jnp.float32) - dot(
        couple_at[last], chain[last].reshape(flat, width), "qm,mn->qn"
    )
    back[last - 1] = route(turned.astype(jnp.bfloat16).reshape(lane_shape), mine_src[last], mine_target[last], block_count)
    for t in reversed(range(1, last)):
        step = back_free(t).astype(jnp.float32) - dot(
            couple_at[t], back[t - 0].reshape(flat, width), "mq,mn->qn"
        )
        back[t - 1] = route(step.astype(jnp.bfloat16).reshape(lane_shape), mine_src[t], mine_target[t], block_count)

    mine_back = solve_backward(solved, own_level_blocks(back[:last] + [zero_block]))
    answer = jnp.where(my_row == last, top, mine_back)
    return (solved[None, None], answer[None, None])


def solution(mesh):
    return jax.shard_map(
        local,
        mesh=mesh,
        in_specs=(
            P("lvl", "blk", None, None),
            P("lvl", "blk", None, None),
            P("lvl", "blk", None, None, None),
            P("lvl", "blk", None, None, None),
            P(),
            P(),
            P(),
        ),
        out_specs=(P("lvl", "blk", None, None), P("lvl", "blk", None, None)),
        check_vma=False,
    )
```

```python
import jax
import jax.numpy as jnp
from jax import lax
from jax.sharding import PartitionSpec as P


def routing_tables(sources, owner, ranks):
    level_count, block_count = owner.shape
    position = jnp.arange(block_count, dtype=jnp.int32)
    tables = [None]
    for t in range(1, level_count):
        at_pos = (owner[t][None, :] == position[:, None]).astype(jnp.int32)
        src_block = jnp.sum(at_pos[:, :, None] * sources[t][None, :, :], axis=1)
        rank_pos = jnp.sum(at_pos[:, :, None] * ranks[t][None, :, :], axis=1)
        pick = (src_block[:, :, None] == position[None, None, :]).astype(jnp.int32)
        src_pos = jnp.sum(pick * owner[t - 1][None, None, :], axis=2)
        hit = (src_pos[:, None, :] == position[None, :, None]).astype(jnp.int32)
        target_of = jnp.sum(hit * position[:, None, None], axis=0)
        tables.append((src_pos, rank_pos, target_of))
    return tables


def mine(table, me):
    block_count = table.shape[0]
    row = (jnp.arange(block_count, dtype=jnp.int32) == me).astype(jnp.int32)
    return jnp.sum(row[:, None] * table, axis=0)


def one_hot(index, count, dtype):
    return (index[:, None] == jnp.arange(count, dtype=jnp.int32)[None, :]).astype(dtype)


def spread(out, src_row, row_count, my_row):
    width = out.shape[-1] // row_count
    piece = None
    for r in range(row_count):
        part = out[..., r * width:(r + 1) * width]
        if r == src_row:
            got = jnp.where(my_row == r, part, jnp.zeros_like(part))
        else:
            got = lax.ppermute(part, "lvl", [(src_row, r)])
        piece = got if piece is None else piece + got
    return piece


def collect(routed, dst_row, row_count):
    parts = []
    for r in range(row_count):
        if r == dst_row:
            parts.append(routed)
        else:
            parts.append(lax.ppermute(routed, "lvl", [(r, dst_row)]))
    return jnp.concatenate(parts, axis=-1)


def shift(array, by, row_count):
    return lax.ppermute(array, "lvl", [(i, (i + by) % row_count) for i in range(row_count)])


def one_hot_rows(index, count, dtype):
    return (jnp.arange(count, dtype=jnp.int32) == index).astype(dtype)


def blocks_of(level_blocks, my_row, by, row_count):
    wanted = lax.rem(my_row + by, row_count)
    chosen = level_blocks[0]
    for t in range(1, len(level_blocks)):
        chosen = jnp.where(wanted == t, level_blocks[t], chosen)
    return chosen


def of_level(parts, index):
    chosen = parts[0]
    for t in range(1, len(parts)):
        chosen = jnp.where(index == t, parts[t], chosen)
    return chosen


def take_block(full, index, count):
    width = full.shape[-1] // count
    blocks = full.reshape(full.shape[:-1] + (count, width))
    hot = (jnp.arange(count, dtype=jnp.int32) == index).astype(full.dtype)
    return jnp.sum(blocks * hot[:, None], axis=-2).astype(full.dtype)


def put_block(part, index, count):
    hot = (jnp.arange(count, dtype=jnp.int32) == index).astype(part.dtype)
    full = part[..., None, :] * hot[:, None]
    return full.reshape(part.shape[:-1] + (count * part.shape[-1],))


def pick_block(blocks, index, count):
    hot = (jnp.arange(count, dtype=jnp.int32) == index).astype(blocks.dtype)
    return jnp.sum(blocks * hot[None, :, None], axis=1).astype(blocks.dtype)


def frees_at(parts, my_row, t, row_count):
    pick = lax.rem(my_row - t + row_count, row_count)
    chosen = parts[0]
    for d in range(1, row_count):
        chosen = jnp.where(pick == d, parts[d], chosen)
    return chosen


def route(piece, send_to, take_from, block_count):
    send = one_hot(send_to, block_count, piece.dtype)
    holder = jnp.einsum("kj,krn->jrn", send, piece, preferred_element_type=jnp.float32)
    holder = holder.astype(piece.dtype)
    arrived = lax.all_to_all(holder, "blk", split_axis=0, concat_axis=0, tiled=True)
    take = one_hot(take_from, block_count, piece.dtype)
    routed = jnp.einsum("kj,jrn->krn", take, arrived, preferred_element_type=jnp.float32)
    return routed.astype(piece.dtype)


def local(rhs, inverse, left_factors, right_factors, sources, ranks, owner):
    assert rhs.shape[1] == 1
    level_count = sources.shape[0]
    block_count = owner.shape[1]
    row_count = lax.axis_size("lvl")
    rank_width = left_factors.shape[4]
    rhs_here = rhs[0, 0]
    inverse_here = inverse[0, 0]
    left_here = left_factors[0, 0]
    right_here = right_factors[0, 0]
    my_row = lax.axis_index("lvl")
    me = lax.axis_index("blk")
    tables = routing_tables(sources, owner, ranks)
    mine_src = [None] + [mine(tables[t][0], me) for t in range(1, level_count)]
    mine_rank = [None] + [mine(tables[t][1], me) for t in range(1, level_count)]
    mine_target = [None] + [mine(tables[t][2], me) for t in range(1, level_count)]
    lanes = jnp.arange(rank_width, dtype=jnp.int32)

    def keep_of(t):
        return (lanes[None, :] < mine_rank[t][:, None]).astype(jnp.float32)

    last = level_count - 1
    tile_count, block_rows, _ = left_here.shape
    columns = rhs_here.shape[-1]
    width = columns // row_count
    flat = tile_count * rank_width
    my_rank = jnp.zeros((tile_count,), jnp.int32)
    for t in range(1, level_count):
        my_rank = jnp.where(my_row == t, mine_rank[t], my_rank)
    keep = (lanes[None, :] < my_rank[:, None]).astype(left_here.dtype)
    left_flat = (left_here * keep[:, None, :]).transpose(1, 0, 2).reshape(block_rows, flat)
    right_flat = right_here.transpose(1, 0, 2).reshape(block_rows, flat)

    def dot(a, b, spec):
        return jnp.einsum(spec, a, b, preferred_element_type=jnp.float32)

    inv_left = dot(inverse_here, left_flat, "ab,bm->am").astype(jnp.bfloat16)
    couple = dot(right_flat, inv_left, "bq,bm->qm").astype(jnp.bfloat16)
    inv_rhs = dot(inverse_here, rhs_here, "ab,bn->an").astype(jnp.bfloat16)
    free = dot(right_flat, inv_rhs, "bq,bn->qn").astype(jnp.bfloat16)
    inv_left_f = inv_left
    gram = dot(inv_left_f, inv_left_f, "bq,bm->qm").astype(jnp.bfloat16)
    turn = dot(inv_left_f, inv_rhs, "bq,bn->qn").astype(jnp.bfloat16)
    couple = jnp.where(my_row == last, gram, couple)
    free = jnp.where(my_row == last, turn, free)
    free_blocks = free.reshape(flat, row_count, width)
    frees = [pick_block(free_blocks, my_row, row_count)]
    for d in range(1, row_count):
        frees.append(shift(pick_block(free_blocks, lax.rem(my_row + d, row_count), row_count), d, row_count))

    def from_row(parts, t):
        pick = lax.rem(my_row - t + row_count, row_count)
        chosen = parts[row_count - 1]
        for d in reversed(range(row_count - 1)):
            chosen = jnp.where(pick == d, parts[d], chosen)
        return chosen

    def solve_forward(coef_full):
        lower = rhs_here.astype(jnp.float32) - dot(
            left_flat, coef_full.reshape(flat, columns), "bm,mn->bn"
        )
        return dot(inverse_here, lower.astype(jnp.bfloat16), "ab,bn->an").astype(jnp.bfloat16)

    def solve_backward(fwd, back_full):
        upper = fwd.astype(jnp.float32) - dot(
            right_flat, back_full.reshape(flat, columns), "bm,mn->bn"
        )
        return dot(inverse_here, upper.astype(jnp.bfloat16), "ba,bn->an").astype(jnp.bfloat16)

    lane_shape = (tile_count, rank_width, width)
    zero_block = jnp.zeros(lane_shape, jnp.bfloat16)

    def own_level_blocks(parts):
        full = put_block(of_level(parts, my_row), my_row, row_count)
        for d in range(1, row_count):
            got = shift(of_level(parts, lax.rem(my_row + d, row_count)), d, row_count)
            full = full + put_block(got, lax.rem(my_row - d + row_count, row_count), row_count)
        return full

    first = inv_rhs
    chain = [zero_block] * level_count
    start_block = frees_at(frees, my_row, 0, row_count).reshape(lane_shape)
    send = one_hot(mine_target[1], block_count, start_block.dtype)
    holder = jnp.einsum("kj,krn->jrn", send, start_block, preferred_element_type=jnp.float32)
    holder = holder.astype(start_block.dtype)
    couples_in, holder = lax.optimization_barrier((couple, holder))
    arrived = lax.all_to_all(holder, "blk", split_axis=0, concat_axis=0, tiled=True)
    take = one_hot(mine_src[1], block_count, start_block.dtype)
    chain[1] = jnp.einsum(
        "kj,jrn->krn", take, arrived, preferred_element_type=jnp.float32
    ).astype(start_block.dtype)
    couples = [couples_in] + [shift(couples_in, d, row_count) for d in range(1, row_count)]
    couple_at = [None] + [from_row(couples, t) for t in range(1, level_count)]
    for t in range(1, last):
        step = frees_at(frees, my_row, t, row_count).astype(jnp.float32) - dot(
            couple_at[t], chain[t].reshape(flat, width), "qm,mn->qn"
        )
        chain[t + 1] = route(step.astype(jnp.bfloat16).reshape(lane_shape), mine_target[t + 1], mine_src[t + 1], block_count)

    lower_chain = [zero_block] + chain[1:last] + [zero_block]
    early_fwd = solve_forward(own_level_blocks(lower_chain))
    inv_t_early = dot(inverse_here, early_fwd, "ba,bn->an").astype(jnp.bfloat16)
    back_term = dot(left_flat, inv_t_early, "bm,bn->mn").astype(jnp.bfloat16)
    top_fwd = solve_forward(collect(chain[last], last, row_count))
    mine_fwd = jnp.where(my_row == last, top_fwd, early_fwd)
    solved = jnp.where(my_row == 0, first, mine_fwd)
    top = dot(inverse_here, solved, "ba,bn->an").astype(jnp.bfloat16)
    back_parts = [take_block(back_term, my_row, row_count)]
    for d in range(1, row_count):
        back_parts.append(shift(take_block(back_term, lax.rem(my_row + d, row_count), row_count), d, row_count))

    def back_free(t):
        return frees_at(back_parts, my_row, t, row_count)

    back = [zero_block] * level_count
    turned = frees_at(frees, my_row, last, row_count).astype(jnp.float32) - dot(
        couple_at[last], chain[last].reshape(flat, width), "qm,mn->qn"
    )
    back[last - 1] = route(turned.astype(jnp.bfloat16).reshape(lane_shape), mine_src[last], mine_target[last], block_count)
    for t in reversed(range(1, last)):
        step = back_free(t).astype(jnp.float32) - dot(
            couple_at[t], back[t - 0].reshape(flat, width), "mq,mn->qn"
        )
        back[t - 1] = route(step.astype(jnp.bfloat16).reshape(lane_shape), mine_src[t], mine_target[t], block_count)

    mine_back = solve_backward(solved, own_level_blocks(back[:last] + [zero_block]))
    answer = jnp.where(my_row == last, top, mine_back)
    return (solved[None, None], answer[None, None])


def solution(mesh):
    return jax.shard_map(
        local,
        mesh=mesh,
        in_specs=(
            P("lvl", "blk", None, None),
            P("lvl", "blk", None, None),
            P("lvl", "blk", None, None, None),
            P("lvl", "blk", None, None, None),
            P(),
            P(),
            P(),
        ),
        out_specs=(P("lvl", "blk", None, None), P("lvl", "blk", None, None)),
        check_vma=False,
    )
```

```python
import jax
import jax.numpy as jnp
from jax import lax
from jax.sharding import PartitionSpec as P


def routing_tables(sources, owner, ranks):
    level_count, block_count = owner.shape
    position = jnp.arange(block_count, dtype=jnp.int32)
    tables = [None]
    for t in range(1, level_count):
        at_pos = (owner[t][None, :] == position[:, None]).astype(jnp.int32)
        src_block = jnp.sum(at_pos[:, :, None] * sources[t][None, :, :], axis=1)
        rank_pos = jnp.sum(at_pos[:, :, None] * ranks[t][None, :, :], axis=1)
        pick = (src_block[:, :, None] == position[None, None, :]).astype(jnp.int32)
        src_pos = jnp.sum(pick * owner[t - 1][None, None, :], axis=2)
        hit = (src_pos[:, None, :] == position[None, :, None]).astype(jnp.int32)
        target_of = jnp.sum(hit * position[:, None, None], axis=0)
        tables.append((src_pos, rank_pos, target_of))
    return tables


def mine(table, me):
    block_count = table.shape[0]
    row = (jnp.arange(block_count, dtype=jnp.int32) == me).astype(jnp.int32)
    return jnp.sum(row[:, None] * table, axis=0)


def one_hot(index, count, dtype):
    return (index[:, None] == jnp.arange(count, dtype=jnp.int32)[None, :]).astype(dtype)


def spread(out, src_row, row_count, my_row):
    width = out.shape[-1] // row_count
    piece = None
    for r in range(row_count):
        part = out[..., r * width:(r + 1) * width]
        if r == src_row:
            got = jnp.where(my_row == r, part, jnp.zeros_like(part))
        else:
            got = lax.ppermute(part, "lvl", [(src_row, r)])
        piece = got if piece is None else piece + got
    return piece


def collect(routed, dst_row, row_count):
    parts = []
    for r in range(row_count):
        if r == dst_row:
            parts.append(routed)
        else:
            parts.append(lax.ppermute(routed, "lvl", [(r, dst_row)]))
    return jnp.concatenate(parts, axis=-1)


def shift(array, by, row_count, senders=None):
    rows = range(row_count) if senders is None else senders
    return lax.ppermute(array, "lvl", [(i, (i + by) % row_count) for i in rows])


def one_hot_rows(index, count, dtype):
    return (jnp.arange(count, dtype=jnp.int32) == index).astype(dtype)


def blocks_of(level_blocks, my_row, by, row_count):
    wanted = lax.rem(my_row + by, row_count)
    chosen = level_blocks[0]
    for t in range(1, len(level_blocks)):
        chosen = jnp.where(wanted == t, level_blocks[t], chosen)
    return chosen


def of_level(parts, index):
    chosen = parts[0]
    for t in range(1, len(parts)):
        chosen = jnp.where(index == t, parts[t], chosen)
    return chosen


def take_block(full, index, count):
    width = full.shape[-1] // count
    blocks = full.reshape(full.shape[:-1] + (count, width))
    hot = (jnp.arange(count, dtype=jnp.int32) == index).astype(full.dtype)
    return jnp.sum(blocks * hot[:, None], axis=-2).astype(full.dtype)


def put_block(part, index, count):
    hot = (jnp.arange(count, dtype=jnp.int32) == index).astype(part.dtype)
    full = part[..., None, :] * hot[:, None]
    return full.reshape(part.shape[:-1] + (count * part.shape[-1],))


def pick_block(blocks, index, count):
    hot = (jnp.arange(count, dtype=jnp.int32) == index).astype(blocks.dtype)
    return jnp.sum(blocks * hot[None, :, None], axis=1).astype(blocks.dtype)


def frees_at(parts, my_row, t, row_count):
    pick = lax.rem(my_row - t + row_count, row_count)
    chosen = parts[0]
    for d in range(1, row_count):
        chosen = jnp.where(pick == d, parts[d], chosen)
    return chosen


def route(piece, send_to, take_from, block_count):
    send = one_hot(send_to, block_count, piece.dtype)
    holder = jnp.einsum("kj,krn->jrn", send, piece, preferred_element_type=jnp.float32)
    holder = holder.astype(piece.dtype)
    arrived = lax.all_to_all(holder, "blk", split_axis=0, concat_axis=0, tiled=True)
    take = one_hot(take_from, block_count, piece.dtype)
    routed = jnp.einsum("kj,jrn->krn", take, arrived, preferred_element_type=jnp.float32)
    return routed.astype(piece.dtype)


def local(rhs, inverse, left_factors, right_factors, sources, ranks, owner):
    assert rhs.shape[1] == 1
    level_count = sources.shape[0]
    block_count = owner.shape[1]
    row_count = lax.axis_size("lvl")
    rank_width = left_factors.shape[4]
    rhs_here = rhs[0, 0]
    inverse_here = inverse[0, 0]
    left_here = left_factors[0, 0]
    right_here = right_factors[0, 0]
    my_row = lax.axis_index("lvl")
    me = lax.axis_index("blk")
    tables = routing_tables(sources, owner, ranks)
    mine_src = [None] + [mine(tables[t][0], me) for t in range(1, level_count)]
    mine_rank = [None] + [mine(tables[t][1], me) for t in range(1, level_count)]
    mine_target = [None] + [mine(tables[t][2], me) for t in range(1, level_count)]
    lanes = jnp.arange(rank_width, dtype=jnp.int32)

    def keep_of(t):
        return (lanes[None, :] < mine_rank[t][:, None]).astype(jnp.float32)

    last = level_count - 1
    tile_count, block_rows, _ = left_here.shape
    columns = rhs_here.shape[-1]
    width = columns // row_count
    flat = tile_count * rank_width
    my_rank = jnp.zeros((tile_count,), jnp.int32)
    for t in range(1, level_count):
        my_rank = jnp.where(my_row == t, mine_rank[t], my_rank)
    keep = (lanes[None, :] < my_rank[:, None]).astype(left_here.dtype)
    left_flat = (left_here * keep[:, None, :]).transpose(1, 0, 2).reshape(block_rows, flat)
    right_flat = right_here.transpose(1, 0, 2).reshape(block_rows, flat)

    def dot(a, b, spec):
        return jnp.einsum(spec, a, b, preferred_element_type=jnp.float32)

    inv_left = dot(inverse_here, left_flat, "ab,bm->am").astype(jnp.bfloat16)
    couple = dot(right_flat, inv_left, "bq,bm->qm").astype(jnp.bfloat16)
    inv_rhs = dot(inverse_here, rhs_here, "ab,bn->an").astype(jnp.bfloat16)
    free = dot(right_flat, inv_rhs, "bq,bn->qn").astype(jnp.bfloat16)
    inv_left_f = inv_left
    gram = dot(inv_left_f, inv_left_f, "bq,bm->qm").astype(jnp.bfloat16)
    turn = dot(inv_left_f, inv_rhs, "bq,bn->qn").astype(jnp.bfloat16)
    couple = jnp.where(my_row == last, gram, couple)
    free = jnp.where(my_row == last, turn, free)
    couples = [couple] + [shift(couple, d, row_count, range(1, row_count)) for d in range(1, row_count)]
    free_blocks = free.reshape(flat, row_count, width)
    frees = [pick_block(free_blocks, my_row, row_count)]
    for d in range(1, row_count):
        frees.append(shift(pick_block(free_blocks, lax.rem(my_row + d, row_count), row_count), d, row_count))

    def from_row(parts, t):
        pick = lax.rem(my_row - t + row_count, row_count)
        chosen = parts[row_count - 1]
        for d in reversed(range(row_count - 1)):
            chosen = jnp.where(pick == d, parts[d], chosen)
        return chosen

    def solve_forward(coef_full):
        lower = rhs_here.astype(jnp.float32) - dot(
            left_flat, coef_full.reshape(flat, columns), "bm,mn->bn"
        )
        return dot(inverse_here, lower.astype(jnp.bfloat16), "ab,bn->an").astype(jnp.bfloat16)

    def solve_backward(fwd, back_full):
        upper = fwd.astype(jnp.float32) - dot(
            right_flat, back_full.reshape(flat, columns), "bm,mn->bn"
        )
        return dot(inverse_here, upper.astype(jnp.bfloat16), "ba,bn->an").astype(jnp.bfloat16)

    lane_shape = (tile_count, rank_width, width)
    zero_block = jnp.zeros(lane_shape, jnp.bfloat16)

    def own_level_blocks(parts):
        full = put_block(of_level(parts, my_row), my_row, row_count)
        for d in range(1, row_count):
            got = shift(of_level(parts, lax.rem(my_row + d, row_count)), d, row_count)
            full = full + put_block(got, lax.rem(my_row - d + row_count, row_count), row_count)
        return full

    first = inv_rhs
    chain = [zero_block] * level_count
    start_block = frees_at(frees, my_row, 0, row_count).reshape(lane_shape)
    chain[1] = route(start_block, mine_target[1], mine_src[1], block_count)
    couple_at = [None] + [from_row(couples, t) for t in range(1, level_count)]
    for t in range(1, last):
        step = frees_at(frees, my_row, t, row_count).astype(jnp.float32) - dot(
            couple_at[t], chain[t].reshape(flat, width), "qm,mn->qn"
        )
        chain[t + 1] = route(step.astype(jnp.bfloat16).reshape(lane_shape), mine_target[t + 1], mine_src[t + 1], block_count)

    lower_chain = [zero_block] + chain[1:last] + [zero_block]
    early_fwd = solve_forward(own_level_blocks(lower_chain))
    inv_t_early = dot(inverse_here, early_fwd, "ba,bn->an").astype(jnp.bfloat16)
    back_term = dot(left_flat, inv_t_early, "bm,bn->mn").astype(jnp.bfloat16)
    top_fwd = solve_forward(collect(chain[last], last, row_count))
    mine_fwd = jnp.where(my_row == last, top_fwd, early_fwd)
    solved = jnp.where(my_row == 0, first, mine_fwd)
    top = dot(inverse_here, solved, "ba,bn->an").astype(jnp.bfloat16)
    back_parts = [take_block(back_term, my_row, row_count)]
    for d in range(1, row_count):
        back_parts.append(shift(take_block(back_term, lax.rem(my_row + d, row_count), row_count), d, row_count, range(1, last)))

    def back_free(t):
        return frees_at(back_parts, my_row, t, row_count)

    back = [zero_block] * level_count
    turned = frees_at(frees, my_row, last, row_count).astype(jnp.float32) - dot(
        couple_at[last], chain[last].reshape(flat, width), "qm,mn->qn"
    )
    back[last - 1] = route(turned.astype(jnp.bfloat16).reshape(lane_shape), mine_src[last], mine_target[last], block_count)
    for t in reversed(range(1, last)):
        step = back_free(t).astype(jnp.float32) - dot(
            couple_at[t], back[t - 0].reshape(flat, width), "mq,mn->qn"
        )
        back[t - 1] = route(step.astype(jnp.bfloat16).reshape(lane_shape), mine_src[t], mine_target[t], block_count)

    mine_back = solve_backward(solved, own_level_blocks(back[:last] + [zero_block]))
    answer = jnp.where(my_row == last, top, mine_back)
    return (solved[None, None], answer[None, None])


def solution(mesh):
    return jax.shard_map(
        local,
        mesh=mesh,
        in_specs=(
            P("lvl", "blk", None, None),
            P("lvl", "blk", None, None),
            P("lvl", "blk", None, None, None),
            P("lvl", "blk", None, None, None),
            P(),
            P(),
            P(),
        ),
        out_specs=(P("lvl", "blk", None, None), P("lvl", "blk", None, None)),
        check_vma=False,
    )
```

```python
import jax
import jax.numpy as jnp
from jax import lax
from jax.sharding import PartitionSpec as P


def routing_tables(sources, owner, ranks):
    level_count, block_count = owner.shape
    position = jnp.arange(block_count, dtype=jnp.int32)
    tables = [None]
    for t in range(1, level_count):
        at_pos = (owner[t][None, :] == position[:, None]).astype(jnp.int32)
        src_block = jnp.sum(at_pos[:, :, None] * sources[t][None, :, :], axis=1)
        rank_pos = jnp.sum(at_pos[:, :, None] * ranks[t][None, :, :], axis=1)
        pick = (src_block[:, :, None] == position[None, None, :]).astype(jnp.int32)
        src_pos = jnp.sum(pick * owner[t - 1][None, None, :], axis=2)
        hit = (src_pos[:, None, :] == position[None, :, None]).astype(jnp.int32)
        target_of = jnp.sum(hit * position[:, None, None], axis=0)
        tables.append((src_pos, rank_pos, target_of))
    return tables


def mine(table, me):
    block_count = table.shape[0]
    row = (jnp.arange(block_count, dtype=jnp.int32) == me).astype(jnp.int32)
    return jnp.sum(row[:, None] * table, axis=0)


def one_hot(index, count, dtype):
    return (index[:, None] == jnp.arange(count, dtype=jnp.int32)[None, :]).astype(dtype)


def spread(out, src_row, row_count, my_row):
    width = out.shape[-1] // row_count
    piece = None
    for r in range(row_count):
        part = out[..., r * width:(r + 1) * width]
        if r == src_row:
            got = jnp.where(my_row == r, part, jnp.zeros_like(part))
        else:
            got = lax.ppermute(part, "lvl", [(src_row, r)])
        piece = got if piece is None else piece + got
    return piece


def collect(routed, dst_row, row_count):
    parts = []
    for r in range(row_count):
        if r == dst_row:
            parts.append(routed)
        else:
            parts.append(lax.ppermute(routed, "lvl", [(r, dst_row)]))
    return jnp.concatenate(parts, axis=-1)


def shift(array, by, row_count):
    return lax.ppermute(array, "lvl", [(i, (i + by) % row_count) for i in range(row_count)])


def one_hot_rows(index, count, dtype):
    return (jnp.arange(count, dtype=jnp.int32) == index).astype(dtype)


def blocks_of(level_blocks, my_row, by, row_count):
    wanted = lax.rem(my_row + by, row_count)
    chosen = level_blocks[0]
    for t in range(1, len(level_blocks)):
        chosen = jnp.where(wanted == t, level_blocks[t], chosen)
    return chosen


def of_level(parts, index):
    chosen = parts[0]
    for t in range(1, len(parts)):
        chosen = jnp.where(index == t, parts[t], chosen)
    return chosen


def take_block(full, index, count):
    width = full.shape[-1] // count
    blocks = full.reshape(full.shape[:-1] + (count, width))
    hot = (jnp.arange(count, dtype=jnp.int32) == index).astype(full.dtype)
    return jnp.sum(blocks * hot[:, None], axis=-2).astype(full.dtype)


def put_block(part, index, count):
    hot = (jnp.arange(count, dtype=jnp.int32) == index).astype(part.dtype)
    full = part[..., None, :] * hot[:, None]
    return full.reshape(part.shape[:-1] + (count * part.shape[-1],))


def pick_block(blocks, index, count):
    hot = (jnp.arange(count, dtype=jnp.int32) == index).astype(blocks.dtype)
    return jnp.sum(blocks * hot[None, :, None], axis=1).astype(blocks.dtype)


def frees_at(parts, my_row, t, row_count):
    pick = lax.rem(my_row - t + row_count, row_count)
    chosen = parts[0]
    for d in range(1, row_count):
        chosen = jnp.where(pick == d, parts[d], chosen)
    return chosen


def route(piece, send_to, take_from, block_count):
    send = one_hot(send_to, block_count, piece.dtype)
    holder = jnp.sum(send[:, :, None, None] * piece[:, None, :, :], axis=0).astype(piece.dtype)
    arrived = lax.all_to_all(holder, "blk", split_axis=0, concat_axis=0, tiled=True)
    take = one_hot(take_from, block_count, piece.dtype)
    routed = jnp.einsum("kj,jrn->krn", take, arrived, preferred_element_type=jnp.float32)
    return routed.astype(piece.dtype)


def local(rhs, inverse, left_factors, right_factors, sources, ranks, owner):
    assert rhs.shape[1] == 1
    level_count = sources.shape[0]
    block_count = owner.shape[1]
    row_count = lax.axis_size("lvl")
    rank_width = left_factors.shape[4]
    rhs_here = rhs[0, 0]
    inverse_here = inverse[0, 0]
    left_here = left_factors[0, 0]
    right_here = right_factors[0, 0]
    my_row = lax.axis_index("lvl")
    me = lax.axis_index("blk")
    tables = routing_tables(sources, owner, ranks)
    mine_src = [None] + [mine(tables[t][0], me) for t in range(1, level_count)]
    mine_rank = [None] + [mine(tables[t][1], me) for t in range(1, level_count)]
    mine_target = [None] + [mine(tables[t][2], me) for t in range(1, level_count)]
    lanes = jnp.arange(rank_width, dtype=jnp.int32)

    def keep_of(t):
        return (lanes[None, :] < mine_rank[t][:, None]).astype(jnp.float32)

    last = level_count - 1
    tile_count, block_rows, _ = left_here.shape
    columns = rhs_here.shape[-1]
    width = columns // row_count
    flat = tile_count * rank_width
    my_rank = jnp.zeros((tile_count,), jnp.int32)
    for t in range(1, level_count):
        my_rank = jnp.where(my_row == t, mine_rank[t], my_rank)
    keep = (lanes[None, :] < my_rank[:, None]).astype(left_here.dtype)
    left_flat = (left_here * keep[:, None, :]).transpose(1, 0, 2).reshape(block_rows, flat)
    right_flat = right_here.transpose(1, 0, 2).reshape(block_rows, flat)

    def dot(a, b, spec):
        return jnp.einsum(spec, a, b, preferred_element_type=jnp.float32)

    inv_left = dot(inverse_here, left_flat, "ab,bm->am").astype(jnp.bfloat16)
    couple = dot(right_flat, inv_left, "bq,bm->qm").astype(jnp.bfloat16)
    inv_rhs = dot(inverse_here, rhs_here, "ab,bn->an").astype(jnp.bfloat16)
    free = dot(right_flat, inv_rhs, "bq,bn->qn").astype(jnp.bfloat16)
    inv_left_f = inv_left
    gram = dot(inv_left_f, inv_left_f, "bq,bm->qm").astype(jnp.bfloat16)
    turn = dot(inv_left_f, inv_rhs, "bq,bn->qn").astype(jnp.bfloat16)
    couple = jnp.where(my_row == last, gram, couple)
    free = jnp.where(my_row == last, turn, free)
    couples = [couple] + [shift(couple, d, row_count) for d in range(1, row_count)]
    free_blocks = free.reshape(flat, row_count, width)
    frees = [pick_block(free_blocks, my_row, row_count)]
    for d in range(1, row_count):
        frees.append(shift(pick_block(free_blocks, lax.rem(my_row + d, row_count), row_count), d, row_count))

    def from_row(parts, t):
        pick = lax.rem(my_row - t + row_count, row_count)
        chosen = parts[row_count - 1]
        for d in reversed(range(row_count - 1)):
            chosen = jnp.where(pick == d, parts[d], chosen)
        return chosen

    def solve_forward(coef_full):
        lower = rhs_here.astype(jnp.float32) - dot(
            left_flat, coef_full.reshape(flat, columns), "bm,mn->bn"
        )
        return dot(inverse_here, lower.astype(jnp.bfloat16), "ab,bn->an").astype(jnp.bfloat16)

    def solve_backward(fwd, back_full):
        upper = fwd.astype(jnp.float32) - dot(
            right_flat, back_full.reshape(flat, columns), "bm,mn->bn"
        )
        return dot(inverse_here, upper.astype(jnp.bfloat16), "ba,bn->an").astype(jnp.bfloat16)

    lane_shape = (tile_count, rank_width, width)
    zero_block = jnp.zeros(lane_shape, jnp.bfloat16)

    def own_level_blocks(parts):
        full = put_block(of_level(parts, my_row), my_row, row_count)
        for d in range(1, row_count):
            got = shift(of_level(parts, lax.rem(my_row + d, row_count)), d, row_count)
            full = full + put_block(got, lax.rem(my_row - d + row_count, row_count), row_count)
        return full

    first = inv_rhs
    chain = [zero_block] * level_count
    start_block = frees_at(frees, my_row, 0, row_count).reshape(lane_shape)
    chain[1] = route(start_block, mine_target[1], mine_src[1], block_count)
    couple_at = [None] + [from_row(couples, t) for t in range(1, level_count)]
    for t in range(1, last):
        step = frees_at(frees, my_row, t, row_count).astype(jnp.float32) - dot(
            couple_at[t], chain[t].reshape(flat, width), "qm,mn->qn"
        )
        chain[t + 1] = route(step.astype(jnp.bfloat16).reshape(lane_shape), mine_target[t + 1], mine_src[t + 1], block_count)

    lower_chain = [zero_block] + chain[1:last] + [zero_block]
    early_fwd = solve_forward(own_level_blocks(lower_chain))
    inv_t_early = dot(inverse_here, early_fwd, "ba,bn->an").astype(jnp.bfloat16)
    back_term = dot(left_flat, inv_t_early, "bm,bn->mn").astype(jnp.bfloat16)
    top_fwd = solve_forward(collect(chain[last], last, row_count))
    mine_fwd = jnp.where(my_row == last, top_fwd, early_fwd)
    solved = jnp.where(my_row == 0, first, mine_fwd)
    top = dot(inverse_here, solved, "ba,bn->an").astype(jnp.bfloat16)
    back_parts = [take_block(back_term, my_row, row_count)]
    for d in range(1, row_count):
        back_parts.append(shift(take_block(back_term, lax.rem(my_row + d, row_count), row_count), d, row_count))

    def back_free(t):
        return frees_at(back_parts, my_row, t, row_count)

    back = [zero_block] * level_count
    turned = frees_at(frees, my_row, last, row_count).astype(jnp.float32) - dot(
        couple_at[last], chain[last].reshape(flat, width), "qm,mn->qn"
    )
    back[last - 1] = route(turned.astype(jnp.bfloat16).reshape(lane_shape), mine_src[last], mine_target[last], block_count)
    for t in reversed(range(1, last)):
        step = back_free(t).astype(jnp.float32) - dot(
            couple_at[t], back[t - 0].reshape(flat, width), "mq,mn->qn"
        )
        back[t - 1] = route(step.astype(jnp.bfloat16).reshape(lane_shape), mine_src[t], mine_target[t], block_count)

    mine_back = solve_backward(solved, own_level_blocks(back[:last] + [zero_block]))
    answer = jnp.where(my_row == last, top, mine_back)
    return (solved[None, None], answer[None, None])


def solution(mesh):
    return jax.shard_map(
        local,
        mesh=mesh,
        in_specs=(
            P("lvl", "blk", None, None),
            P("lvl", "blk", None, None),
            P("lvl", "blk", None, None, None),
            P("lvl", "blk", None, None, None),
            P(),
            P(),
            P(),
        ),
        out_specs=(P("lvl", "blk", None, None), P("lvl", "blk", None, None)),
        check_vma=False,
    )
```
